512 devices in a mesh: wide: 64 (over z, x, core), narrow: 8 (over y).
Axes of the slice: x: 4, y: 8, z: 8, core: 2. Of those that a mesh axis runs over, the one named last changes fastest.
Arguments:
- hidden_in: bfloat16 [16384, 2048], P('wide', 'narrow'), may hold values from -6 to 6
- segment_ids: int32 [16384], P('wide'), may hold values from 0 to 31, never falling along the last dimension, each value on 1 to 2048 neighbouring positions
- page_table: int32 [1024], P('wide'), may hold values from 0 to 1023, as said below
- wq: bfloat16 [2048, 2048], P('wide', 'narrow')
- wk: bfloat16 [2048, 2048], P('wide', 'narrow')
- wv: bfloat16 [2048, 2048], P('wide', 'narrow'), may hold values from -0.125 to 0.125
- wo: bfloat16 [2048, 2048], P('narrow', 'wide'), may hold values from -0.125 to 0.125
- wg: bfloat16 [2048, 4096], P('wide', 'narrow'), may hold values from -0.125 to 0.125
- wu: bfloat16 [2048, 4096], P('wide', 'narrow'), may hold values from -0.125 to 0.125
- wd: bfloat16 [4096, 2048], P('narrow', 'wide'), may hold values from -0.09375 to 0.09375
Outputs:
- result: bfloat16 [16384, 2048], P('wide', 'narrow')
- kv_cache: bfloat16 [2, 1024, 16, 2048], P(None, 'wide', None, 'narrow')
The draws below stay inside these ranges and needn't reach their ends.
Inputs may be any that keep to these rules, and one draw needn't show every extreme that they name: `page_table`: entries 16 * w to 16 * (w + 1) - 1 of the table are a permutation of those same numbers, for every w.
All inputs are finite; a program needn't handle non-finite values.
Results may differ from the reference program's by a relative error of at most 0.017.
Values may be sent and summed in bfloat16 or wider, within the bound.
No kernel may reach another device: no remote copies, remote signals or barrier semaphores. Data moves between devices by JAX's collectives and lax.ppermute only.
A program may use at most 64 MiB of HBM per device.

```python
import math
import jax
import jax.numpy as jnp
import numpy as np
from jax import lax

D = 2048
HEADS = 16
HEAD_DIM = 128
FF = 4096
TOK_DEV = 256
REACH = 8
PAGE = 16
TOKENS = 16384
MAXLEN = 2048
NSEG = 32
PAGES_DEV = 16
NPAGE = 1024
N_NARROW = 8


def shared_projections(key):
    base_draw = jax.random.normal(jax.random.fold_in(key, 11), (D, HEADS * HEAD_DIM), jnp.float32) * D ** (-0.5)
    other_draw = jax.random.normal(jax.random.fold_in(key, 12), (D, HEADS * HEAD_DIM), jnp.float32) * D ** (-0.5)
    return (base_draw, other_draw)


def draw_wq(key, part):
    return shared_projections(key)[0].astype(jnp.bfloat16)


def draw_wk(key, part):
    return shared_projections(key)[1].astype(jnp.bfloat16)


def draw_page_table(key, part):
    block_count = NPAGE // PAGES_DEV
    key_list = jax.random.split(jax.random.fold_in(key, 5), block_count)

    def one_block(block_key):
        return jax.random.permutation(block_key, PAGES_DEV)
    shuffled = jax.vmap(one_block)(key_list).astype(jnp.int32)
    offsets = jnp.arange(block_count, dtype=jnp.int32)[:, None] * PAGES_DEV
    return (shuffled + offsets).reshape(NPAGE)


def steps_of(own_key, extent, shards, smallest, top_value):
    def one(dim, shards_of):
        steps = jax.random.uniform(jax.random.fold_in(jax.random.fold_in(own_key, 6), dim), (shards_of,), jnp.float32, smallest / len(shards), top_value / len(shards))
        return jnp.repeat(jnp.exp(steps), extent[dim] // shards_of).reshape((-1,) + (1,) * (len(extent) - dim - 1))

    level = one(*shards[0])
    for cut in shards[1:]:
        level = level * one(*cut)
    return level


def profile(amount, total, limit, skew):
    loads = [(1 << 20) // math.isqrt(standing ** skew) + 1 for standing in range(2, amount + 1)]
    surplus, given = total - limit - (amount - 1), [1] * (amount - 1)
    while surplus > 0:
        movable = [i for i in range(amount - 1) if given[i] < limit]
        mass, remaining = sum([loads[i] for i in movable]), surplus
        for i in movable:
            extra = min(limit - given[i], max(1, remaining * loads[i] // mass), surplus)
            given[i] = given[i] + extra
            surplus = surplus - extra
    return np.array([limit] + given)


def uneven(key, amount, total, limit, skew):
    if amount == 2:
        one = jax.random.randint(key, (), max(1, total - limit), min(limit, total - 1) + 1)
        return jnp.stack([one, total - one])
    lengths = jnp.asarray(profile(amount, total, limit, skew), jnp.int32)
    couples = (amount - 1) // 2
    source_of, receiver = lengths[1:1 + 2 * couples:2], lengths[2:2 + 2 * couples:2]
    slack = jnp.minimum(source_of - 1, limit - receiver)
    passed = jax.random.randint(jax.random.fold_in(key, 1), (couples,), 0, 1 << 20) % (slack + 1)
    lengths = lengths.at[1:1 + 2 * couples:2].set(source_of - passed).at[2:2 + 2 * couples:2].set(receiver + passed)
    return lengths[jax.random.permutation(jax.random.fold_in(key, 2), amount)]


def gaussian(stream_key, extent, scale, bound, pieces=(), kind=jnp.bfloat16):
    drawn = jax.random.normal(stream_key, extent, jnp.float32) * scale
    if len(pieces) > 0:
        drawn = steps_of(stream_key, extent, pieces, -0.22, 0.18) * drawn
    return jnp.clip(drawn, min=-bound, max=bound).astype(kind)


def setup_inputs(seed: int = 0) -> dict:
    splits = jax.random.split(jax.random.key(seed), 11)
    hidden_in = gaussian(splits[0], (TOKENS, D), 1.0, 6.0, ((0, 64), (1, 8)))
    segment_ids = jnp.searchsorted(jnp.cumsum(uneven(splits[1], NSEG, TOKENS, MAXLEN, 2)), jnp.arange(TOKENS), side="right").astype(jnp.int32)
    page_table = draw_page_table(jax.random.fold_in(splits[10], 71), 0)
    wq = draw_wq(jax.random.fold_in(splits[10], 71), 0)
    wk = draw_wk(jax.random.fold_in(splits[10], 71), 0)
    wv = gaussian(splits[5], (D, HEADS * HEAD_DIM), D ** -0.5, 0.125, ((0, 64), (1, 8)))
    wo = gaussian(splits[6], (HEADS * HEAD_DIM, D), (HEADS * HEAD_DIM) ** -0.5, 0.125, ((0, 8), (1, 64)))
    wg = gaussian(splits[7], (D, FF), D ** -0.5, 0.125, ((0, 64), (1, 8)))
    wu = gaussian(splits[8], (D, FF), D ** -0.5, 0.125, ((0, 64), (1, 8)))
    wd = gaussian(splits[9], (FF, D), FF ** -0.5, 0.09375, ((0, 8), (1, 64)))
    return dict(hidden_in=hidden_in, segment_ids=segment_ids, page_table=page_table, wq=wq, wk=wk, wv=wv, wo=wo, wg=wg, wu=wu, wd=wd)


epsilon = 1e-05
rope_base = 10000.0

def norm_rows(source):
    widened = source.astype(jnp.float32)
    center = widened - lax.optimization_barrier(jnp.mean(widened, axis=-1, keepdims=True))
    spread = lax.optimization_barrier(jnp.mean(center * center, axis=-1, keepdims=True))
    return (center * lax.rsqrt(spread + epsilon)).astype(jnp.bfloat16)

def rotate(projected, positions):
    head_size = projected.shape[-1]
    half_dim = head_size // 2
    frequency = jnp.power(rope_base, -jnp.arange(half_dim, dtype=jnp.float32) * 2.0 / head_size)
    angles = positions.astype(jnp.float32)[:, None] * frequency[None, :]
    cosine = jnp.cos(angles)[:, None, :]
    sine_part = jnp.sin(angles)[:, None, :]
    first_half = projected[..., :half_dim]
    second_half = projected[..., half_dim:]
    return jnp.concatenate([first_half * cosine - second_half * sine_part, second_half * cosine + first_half * sine_part], axis=-1)

def grouped(left_side, right_side):
    group_size = left_side.shape[1] // N_NARROW
    running = jnp.zeros((left_side.shape[0], right_side.shape[1]), jnp.float32)
    for member in range(N_NARROW):
        part_sum = jnp.dot(left_side[:, member * group_size:(member + 1) * group_size], right_side[member * group_size:(member + 1) * group_size], preferred_element_type=jnp.float32)
        rounded = lax.optimization_barrier(part_sum.astype(jnp.bfloat16))
        running = running + rounded.astype(jnp.float32)
    return running

def reference(hidden_in, segment_ids, page_table, wq, wk, wv, wo, wg, wu, wd):
    total_rows = hidden_in.shape[0]
    width_all = HEADS * HEAD_DIM
    slot_index = jnp.arange(total_rows, dtype=jnp.int32)
    counts = jax.ops.segment_sum(jnp.ones_like(segment_ids), segment_ids, num_segments=NSEG)
    starts = (jnp.cumsum(counts) - counts).astype(jnp.int32)
    positions = slot_index - starts[segment_ids]
    normed = norm_rows(hidden_in)
    queries = rotate(jnp.dot(normed, wq, preferred_element_type=jnp.float32).reshape(total_rows, HEADS, HEAD_DIM), positions).astype(jnp.bfloat16)
    keys_rot = rotate(jnp.dot(normed, wk, preferred_element_type=jnp.float32).reshape(total_rows, HEADS, HEAD_DIM), positions).astype(jnp.bfloat16)
    values = jnp.dot(normed, wv, preferred_element_type=jnp.float32).astype(jnp.bfloat16).reshape(total_rows, HEADS, HEAD_DIM)
    window = (REACH + 1) * TOK_DEV
    lead_rows = REACH * TOK_DEV
    keys_padded = jnp.concatenate([jnp.zeros((lead_rows, HEADS, HEAD_DIM), jnp.bfloat16), keys_rot], axis=0)
    values_padded = jnp.concatenate([jnp.zeros((lead_rows, HEADS, HEAD_DIM), jnp.bfloat16), values], axis=0)
    score_scale = HEAD_DIM ** (-0.5)

    def attend(block_id):
        block_first = block_id * TOK_DEV
        query_blk = lax.dynamic_slice_in_dim(queries, block_first, TOK_DEV, 0)
        key_blk = lax.dynamic_slice_in_dim(keys_padded, block_first, window, 0)
        value_blk = lax.dynamic_slice_in_dim(values_padded, block_first, window, 0)
        query_index = block_first + jnp.arange(TOK_DEV, dtype=jnp.int32)
        key_index = block_first - lead_rows + jnp.arange(window, dtype=jnp.int32)
        query_start = query_index - lax.dynamic_slice_in_dim(positions, block_first, TOK_DEV, 0)
        allowed = (key_index[None, :] >= query_start[:, None]) & (key_index[None, :] <= query_index[:, None])
        scores = jnp.einsum('qhd,khd->hqk', query_blk.astype(jnp.float32), key_blk.astype(jnp.float32)) * score_scale
        scores = jnp.where(allowed[None], scores, -1e+30)
        row_peak = lax.optimization_barrier(jnp.max(scores, axis=-1, keepdims=True))
        exps = jnp.where(allowed[None], jnp.exp(scores - row_peak), 0.0)
        attn_probs = (exps / lax.optimization_barrier(jnp.sum(exps, axis=-1, keepdims=True))).astype(jnp.bfloat16)
        mixed = jnp.einsum('hqk,khd->qhd', attn_probs.astype(jnp.float32), value_blk.astype(jnp.float32))
        return mixed.astype(jnp.bfloat16).reshape(TOK_DEV, width_all)
    attended = lax.map(attend, jnp.arange(total_rows // TOK_DEV, dtype=jnp.int32)).reshape(total_rows, width_all)
    first_res = (hidden_in.astype(jnp.float32) + grouped(attended, wo)).astype(jnp.bfloat16)
    normed_two = norm_rows(first_res)
    gate_proj = jnp.dot(normed_two, wg, preferred_element_type=jnp.float32)
    up_proj = jnp.dot(normed_two, wu, preferred_element_type=jnp.float32)
    hidden = (jax.nn.silu(gate_proj) * up_proj).astype(jnp.bfloat16)
    result = (first_res.astype(jnp.float32) + grouped(hidden, wd)).astype(jnp.bfloat16)
    cache_pairs = jnp.stack([keys_rot.reshape(NPAGE, PAGE, width_all), values.reshape(NPAGE, PAGE, width_all)], axis=0)
    kv_cache = jnp.zeros_like(cache_pairs).at[:, page_table].set(cache_pairs)
    return (result, kv_cache)
```

```python
import jax
import jax.numpy as jnp
from jax import lax
from jax.sharding import PartitionSpec as P

HEAD_DIM = 128
REACH = 8
PAGE = 16


epsilon = 1e-05
rope_base = 10000.0


def shifted(value, axis, steps):
    count = lax.axis_size(axis)
    first, last = (max(0, -steps), min(count, count - steps))
    return lax.ppermute(value, axis, [(source, source + steps) for source in range(first, last)])


def norm_rows(source):
    widened = source.astype(jnp.float32)
    center = widened - jnp.mean(widened, axis=-1, keepdims=True)
    spread = jnp.mean(center * center, axis=-1, keepdims=True)
    return (center * lax.rsqrt(spread + epsilon)).astype(jnp.bfloat16)


def rotate(projected, positions):
    head_size = projected.shape[-1]
    half_dim = head_size // 2
    frequency = jnp.power(rope_base, -jnp.arange(half_dim, dtype=jnp.float32) * 2.0 / head_size)
    angles = positions.astype(jnp.float32)[:, None] * frequency[None, :]
    cosine = jnp.cos(angles)[:, None, :]
    sine_part = jnp.sin(angles)[:, None, :]
    first_half = projected[..., :half_dim]
    second_half = projected[..., half_dim:]
    return jnp.concatenate(
        [
            first_half * cosine - second_half * sine_part,
            second_half * cosine + first_half * sine_part,
        ],
        axis=-1,
    )


def add_rows(source, piece):
    return jnp.dot(source, piece, preferred_element_type=jnp.float32)


def per_device(hidden_in, segment_ids, page_table, wq, wk, wv, wo, wg, wu, wd):
    tok_rows = hidden_in.shape[0]
    wide_rank = lax.axis_index("wide")
    local_index = jnp.arange(tok_rows, dtype=jnp.int32)

    attn_width = wq.shape[1]
    ff_width = wg.shape[1]
    pieces = [wq, wk, wv, wo.T, wg, wu, wd.T]
    widths = [piece.shape[1] for piece in pieces]
    gathered = lax.all_gather(jnp.concatenate(pieces, axis=1), "wide", axis=0, tiled=True)
    offsets = [sum(widths[:k]) for k in range(len(widths))]
    full = [gathered[:, o:o + w] for o, w in zip(offsets, widths)]
    wq_all, wk_all, wv_all, wo_t, wg_all, wu_all, wd_t = full

    id_blocks = []
    for step_back in range(REACH, 0, -1):
        got = shifted(segment_ids, "wide", step_back)
        id_blocks.append(jnp.where(wide_rank >= step_back, got, -1))
    id_blocks.append(segment_ids)
    window_ids = jnp.concatenate(id_blocks, axis=0)
    window_len = window_ids.shape[0]
    lead = REACH * tok_rows
    window_index = jnp.arange(window_len, dtype=jnp.int32)
    same = window_ids[None, :] == segment_ids[:, None]
    allowed = same & (window_index[None, :] <= lead + local_index[:, None])
    earlier = same & (window_index[None, :] < lead + local_index[:, None])
    positions = jnp.sum(earlier.astype(jnp.int32), axis=1)

    whole = lax.all_gather(hidden_in, "narrow", axis=1, tiled=True)
    normed = norm_rows(whole)
    local_width = attn_width
    head_count = local_width // HEAD_DIM

    q_proj = add_rows(normed, wq_all)
    k_proj = add_rows(normed, wk_all)
    v_proj = add_rows(normed, wv_all)
    queries = rotate(q_proj.reshape(tok_rows, head_count, HEAD_DIM), positions).astype(jnp.bfloat16)
    keys_rot = rotate(k_proj.reshape(tok_rows, head_count, HEAD_DIM), positions).astype(
        jnp.bfloat16
    )
    values = v_proj.astype(jnp.bfloat16).reshape(tok_rows, head_count, HEAD_DIM)
    blocks = []
    for step_back in range(REACH, 0, -1):
        blocks.append(shifted((keys_rot, values), "wide", step_back))
    blocks.append((keys_rot, values))
    score_scale = HEAD_DIM ** (-0.5)
    key_all = jnp.concatenate([member[0] for member in blocks], axis=0)
    value_all = jnp.concatenate([member[1] for member in blocks], axis=0)
    scores = (
        jnp.einsum("qhd,khd->hqk", queries, key_all, preferred_element_type=jnp.float32)
        * score_scale
    )
    scores = jnp.where(allowed[None], scores, -1e30)
    row_peak = jnp.max(scores, axis=-1, keepdims=True)
    exps = jnp.where(allowed[None], jnp.exp(scores - row_peak), 0.0)
    attn_probs = (exps / jnp.sum(exps, axis=-1, keepdims=True)).astype(jnp.bfloat16)
    mixed = jnp.einsum("hqk,khd->qhd", attn_probs, value_all, preferred_element_type=jnp.float32)
    attended = mixed.astype(jnp.bfloat16).reshape(tok_rows, local_width)
    attn_terms = lax.dot_general(
        attended, wo_t, (((1,), (1,)), ((), ())), preferred_element_type=jnp.float32
    )
    attn_sum = lax.psum_scatter(
        attn_terms.astype(jnp.bfloat16), "narrow", scatter_dimension=1, tiled=True
    ).astype(jnp.float32)
    first_res = (hidden_in.astype(jnp.float32) + attn_sum).astype(jnp.bfloat16)
    whole_two = lax.all_gather(first_res, "narrow", axis=1, tiled=True)
    normed_two = norm_rows(whole_two)

    gate_proj = add_rows(normed_two, wg_all)
    up_proj = add_rows(normed_two, wu_all)
    hidden = (jax.nn.silu(gate_proj) * up_proj).astype(jnp.bfloat16)
    down_terms = lax.dot_general(
        hidden, wd_t, (((1,), (1,)), ((), ())), preferred_element_type=jnp.float32
    )
    down_sum = lax.psum_scatter(
        down_terms.astype(jnp.bfloat16), "narrow", scatter_dimension=1, tiled=True
    ).astype(jnp.float32)
    result = (first_res.astype(jnp.float32) + down_sum).astype(jnp.bfloat16)
    page_count = tok_rows // PAGE
    slots = page_table - wide_rank * page_count
    pairs = jnp.stack(
        [
            keys_rot.reshape(page_count, PAGE, local_width),
            values.reshape(page_count, PAGE, local_width),
        ],
        axis=0,
    )
    kv_cache = jnp.zeros_like(pairs).at[:, slots].set(pairs)
    return (result, kv_cache)


def solution(mesh):
    return jax.shard_map(
        per_device,
        mesh=mesh,
        in_specs=(
            P("wide", "narrow"),
            P("wide"),
            P("wide"),
            P("wide", "narrow"),
            P("wide", "narrow"),
            P("wide", "narrow"),
            P("narrow", "wide"),
            P("wide", "narrow"),
            P("wide", "narrow"),
            P("narrow", "wide"),
        ),
        out_specs=(P("wide", "narrow"), P(None, "wide", None, "narrow")),
        check_vma=False,
    )
```

```python
import jax
import jax.numpy as jnp
from jax import lax
from jax.sharding import PartitionSpec as P

HEAD_DIM = 128
REACH = 8
PAGE = 16


epsilon = 1e-05
rope_base = 10000.0


def shifted(value, axis, steps):
    count = lax.axis_size(axis)
    first, last = (max(0, -steps), min(count, count - steps))
    return lax.ppermute(value, axis, [(source, source + steps) for source in range(first, last)])


def ring_gather(value, axis, dim):
    count, mine = (lax.axis_size(axis), lax.axis_index(axis))
    got = [value]
    for steps in range(1, count):
        got.append(lax.ppermute(value, axis, [(source, (source + steps) % count) for source in range(count)]))
    stacked = jnp.stack(got, axis=0)
    order = (mine - jnp.arange(count, dtype=jnp.int32)) % count
    ordered = jnp.take(stacked, order, axis=0)
    ordered = jnp.moveaxis(ordered, 0, dim)
    shape = list(value.shape)
    shape[dim] = shape[dim] * count
    return ordered.reshape(shape)


def norm_rows(source):
    widened = source.astype(jnp.float32)
    center = widened - jnp.mean(widened, axis=-1, keepdims=True)
    spread = jnp.mean(center * center, axis=-1, keepdims=True)
    return (center * lax.rsqrt(spread + epsilon)).astype(jnp.bfloat16)


def rotate(projected, positions):
    head_size = projected.shape[-1]
    half_dim = head_size // 2
    frequency = jnp.power(rope_base, -jnp.arange(half_dim, dtype=jnp.float32) * 2.0 / head_size)
    angles = positions.astype(jnp.float32)[:, None] * frequency[None, :]
    cosine = jnp.cos(angles)[:, None, :]
    sine_part = jnp.sin(angles)[:, None, :]
    first_half = projected[..., :half_dim]
    second_half = projected[..., half_dim:]
    return jnp.concatenate(
        [
            first_half * cosine - second_half * sine_part,
            second_half * cosine + first_half * sine_part,
        ],
        axis=-1,
    )


def add_rows(source, piece):
    return jnp.dot(source, piece, preferred_element_type=jnp.float32)


def per_device(hidden_in, segment_ids, page_table, wq, wk, wv, wo, wg, wu, wd):
    tok_rows = hidden_in.shape[0]
    wide_rank = lax.axis_index("wide")
    local_index = jnp.arange(tok_rows, dtype=jnp.int32)

    attn_width = wq.shape[1]
    ff_width = wg.shape[1]
    pieces = [wq, wk, wv, wo.T, wg, wu, wd.T]
    widths = [piece.shape[1] for piece in pieces]
    gathered = lax.all_gather(jnp.concatenate(pieces, axis=1), "wide", axis=0, tiled=True)
    offsets = [sum(widths[:k]) for k in range(len(widths))]
    full = [gathered[:, o:o + w] for o, w in zip(offsets, widths)]
    wq_all, wk_all, wv_all, wo_t, wg_all, wu_all, wd_t = full

    id_blocks = []
    for step_back in range(REACH, 0, -1):
        got = shifted(segment_ids, "wide", step_back)
        id_blocks.append(jnp.where(wide_rank >= step_back, got, -1))
    id_blocks.append(segment_ids)
    window_ids = jnp.concatenate(id_blocks, axis=0)
    window_len = window_ids.shape[0]
    lead = REACH * tok_rows
    window_index = jnp.arange(window_len, dtype=jnp.int32)
    same = window_ids[None, :] == segment_ids[:, None]
    allowed = same & (window_index[None, :] <= lead + local_index[:, None])
    earlier = same & (window_index[None, :] < lead + local_index[:, None])
    positions = jnp.sum(earlier.astype(jnp.int32), axis=1)

    whole = ring_gather(hidden_in, "narrow", 1)
    normed = norm_rows(whole)
    local_width = attn_width
    head_count = local_width // HEAD_DIM

    q_proj = add_rows(normed, wq_all)
    k_proj = add_rows(normed, wk_all)
    v_proj = add_rows(normed, wv_all)
    queries = rotate(q_proj.reshape(tok_rows, head_count, HEAD_DIM), positions).astype(jnp.bfloat16)
    keys_rot = rotate(k_proj.reshape(tok_rows, head_count, HEAD_DIM), positions).astype(
        jnp.bfloat16
    )
    values = v_proj.astype(jnp.bfloat16).reshape(tok_rows, head_count, HEAD_DIM)
    packed = jnp.concatenate([keys_rot, values], axis=2)
    blocks = []
    for step_back in range(REACH, 0, -1):
        blocks.append(shifted(packed, "wide", step_back))
    blocks.append(packed)
    score_scale = HEAD_DIM ** (-0.5)
    kv_all = jnp.concatenate(blocks, axis=0)
    key_all = kv_all[:, :, :HEAD_DIM]
    value_all = kv_all[:, :, HEAD_DIM:]
    scores = (
        jnp.einsum("qhd,khd->hqk", queries, key_all, preferred_element_type=jnp.float32)
        * score_scale
    )
    scores = jnp.where(allowed[None], scores, -1e30)
    row_peak = jnp.max(scores, axis=-1, keepdims=True)
    exps = jnp.where(allowed[None], jnp.exp(scores - row_peak), 0.0)
    attn_probs = (exps / jnp.sum(exps, axis=-1, keepdims=True)).astype(jnp.bfloat16)
    mixed = jnp.einsum("hqk,khd->qhd", attn_probs, value_all, preferred_element_type=jnp.float32)
    attended = mixed.astype(jnp.bfloat16).reshape(tok_rows, local_width)
    attn_terms = lax.dot_general(
        attended, wo_t, (((1,), (1,)), ((), ())), preferred_element_type=jnp.float32
    )
    attn_sum = lax.psum(attn_terms.astype(jnp.bfloat16), "narrow").astype(jnp.float32)
    whole_two = (whole.astype(jnp.float32) + attn_sum).astype(jnp.bfloat16)
    narrow_rank = lax.axis_index("narrow")
    feat = hidden_in.shape[1]
    first_res = lax.dynamic_slice_in_dim(whole_two, narrow_rank * feat, feat, axis=1)
    normed_two = norm_rows(whole_two)

    gate_proj = add_rows(normed_two, wg_all)
    up_proj = add_rows(normed_two, wu_all)
    hidden = (jax.nn.silu(gate_proj) * up_proj).astype(jnp.bfloat16)
    down_terms = lax.dot_general(
        hidden, wd_t, (((1,), (1,)), ((), ())), preferred_element_type=jnp.float32
    )
    down_sum = lax.psum_scatter(
        down_terms.astype(jnp.bfloat16), "narrow", scatter_dimension=1, tiled=True
    ).astype(jnp.float32)
    result = (first_res.astype(jnp.float32) + down_sum).astype(jnp.bfloat16)
    page_count = tok_rows // PAGE
    slots = page_table - wide_rank * page_count
    pairs = jnp.stack(
        [
            keys_rot.reshape(page_count, PAGE, local_width),
            values.reshape(page_count, PAGE, local_width),
        ],
        axis=0,
    )
    kv_cache = jnp.zeros_like(pairs).at[:, slots].set(pairs)
    return (result, kv_cache)


def solution(mesh):
    return jax.shard_map(
        per_device,
        mesh=mesh,
        in_specs=(
            P("wide", "narrow"),
            P("wide"),
            P("wide"),
            P("wide", "narrow"),
            P("wide", "narrow"),
            P("wide", "narrow"),
            P("narrow", "wide"),
            P("wide", "narrow"),
            P("wide", "narrow"),
            P("narrow", "wide"),
        ),
        out_specs=(P("wide", "narrow"), P(None, "wide", None, "narrow")),
        check_vma=False,
    )
```

```python
import jax
import jax.numpy as jnp
from jax import lax
from jax.sharding import PartitionSpec as P

HEAD_DIM = 128
REACH = 8
PAGE = 16


epsilon = 1e-05
rope_base = 10000.0


def shifted(value, axis, steps):
    count = lax.axis_size(axis)
    first, last = (max(0, -steps), min(count, count - steps))
    return lax.ppermute(value, axis, [(source, source + steps) for source in range(first, last)])


def swap_gather(value, axis):
    count = lax.axis_size(axis)
    rows, cols = value.shape
    copies = jnp.broadcast_to(value[None], (count, rows, cols))
    got = lax.all_to_all(copies, axis, 0, 0, tiled=True)
    return jnp.moveaxis(got, 0, 1).reshape(rows, cols * count)


def swap_sum(value, axis):
    count = lax.axis_size(axis)
    rows, width = value.shape
    cols = width // count
    pieces = jnp.moveaxis(value.reshape(rows, count, cols), 1, 0)
    got = lax.all_to_all(pieces, axis, 0, 0, tiled=True)
    return jnp.sum(got.astype(jnp.float32), axis=0)


def norm_rows(source):
    widened = source.astype(jnp.float32)
    center = widened - jnp.mean(widened, axis=-1, keepdims=True)
    spread = jnp.mean(center * center, axis=-1, keepdims=True)
    return (center * lax.rsqrt(spread + epsilon)).astype(jnp.bfloat16)


def rotate(projected, positions):
    head_size = projected.shape[-1]
    half_dim = head_size // 2
    frequency = jnp.power(rope_base, -jnp.arange(half_dim, dtype=jnp.float32) * 2.0 / head_size)
    angles = positions.astype(jnp.float32)[:, None] * frequency[None, :]
    cosine = jnp.cos(angles)[:, None, :]
    sine_part = jnp.sin(angles)[:, None, :]
    first_half = projected[..., :half_dim]
    second_half = projected[..., half_dim:]
    return jnp.concatenate(
        [
            first_half * cosine - second_half * sine_part,
            second_half * cosine + first_half * sine_part,
        ],
        axis=-1,
    )


def add_rows(source, piece):
    return jnp.dot(source, piece, preferred_element_type=jnp.float32)


def per_device(hidden_in, segment_ids, page_table, wq, wk, wv, wo, wg, wu, wd):
    tok_rows = hidden_in.shape[0]
    wide_rank = lax.axis_index("wide")
    local_index = jnp.arange(tok_rows, dtype=jnp.int32)

    attn_width = wq.shape[1]
    ff_width = wg.shape[1]
    pieces = [wq, wk, wv, wo.T, wg, wu, wd.T]
    widths = [piece.shape[1] for piece in pieces]
    gathered = lax.all_gather(jnp.concatenate(pieces, axis=1), "wide", axis=0, tiled=True)
    offsets = [sum(widths[:k]) for k in range(len(widths))]
    full = [gathered[:, o:o + w] for o, w in zip(offsets, widths)]
    wq_all, wk_all, wv_all, wo_t, wg_all, wu_all, wd_t = full

    id_blocks = []
    for step_back in range(REACH, 0, -1):
        got = shifted(segment_ids, "wide", step_back)
        id_blocks.append(jnp.where(wide_rank >= step_back, got, -1))
    id_blocks.append(segment_ids)
    window_ids = jnp.concatenate(id_blocks, axis=0)
    window_len = window_ids.shape[0]
    lead = REACH * tok_rows
    window_index = jnp.arange(window_len, dtype=jnp.int32)
    same = window_ids[None, :] == segment_ids[:, None]
    allowed = same & (window_index[None, :] <= lead + local_index[:, None])
    earlier = same & (window_index[None, :] < lead + local_index[:, None])
    positions = jnp.sum(earlier.astype(jnp.int32), axis=1)

    whole = swap_gather(hidden_in, "narrow")
    normed = norm_rows(whole)
    local_width = attn_width
    head_count = local_width // HEAD_DIM

    q_proj = add_rows(normed, wq_all)
    k_proj = add_rows(normed, wk_all)
    v_proj = add_rows(normed, wv_all)
    queries = rotate(q_proj.reshape(tok_rows, head_count, HEAD_DIM), positions).astype(jnp.bfloat16)
    keys_rot = rotate(k_proj.reshape(tok_rows, head_count, HEAD_DIM), positions).astype(
        jnp.bfloat16
    )
    values = v_proj.astype(jnp.bfloat16).reshape(tok_rows, head_count, HEAD_DIM)
    packed = jnp.concatenate([keys_rot, values], axis=2)
    blocks = []
    for step_back in range(REACH, 0, -1):
        blocks.append(shifted(packed, "wide", step_back))
    blocks.append(packed)
    score_scale = HEAD_DIM ** (-0.5)
    kv_all = jnp.concatenate(blocks, axis=0)
    key_all = kv_all[:, :, :HEAD_DIM]
    value_all = kv_all[:, :, HEAD_DIM:]
    scores = (
        jnp.einsum("qhd,khd->hqk", queries, key_all, preferred_element_type=jnp.float32)
        * score_scale
    )
    scores = jnp.where(allowed[None], scores, -1e30)
    row_peak = jnp.max(scores, axis=-1, keepdims=True)
    exps = jnp.where(allowed[None], jnp.exp(scores - row_peak), 0.0)
    attn_probs = (exps / jnp.sum(exps, axis=-1, keepdims=True)).astype(jnp.bfloat16)
    mixed = jnp.einsum("hqk,khd->qhd", attn_probs, value_all, preferred_element_type=jnp.float32)
    attended = mixed.astype(jnp.bfloat16).reshape(tok_rows, local_width)
    attn_terms = lax.dot_general(
        attended, wo_t, (((1,), (1,)), ((), ())), preferred_element_type=jnp.float32
    )
    attn_sum = swap_sum(attn_terms.astype(jnp.bfloat16), "narrow")
    first_res = (hidden_in.astype(jnp.float32) + attn_sum).astype(jnp.bfloat16)
    whole_two = swap_gather(first_res, "narrow")
    normed_two = norm_rows(whole_two)

    gate_proj = add_rows(normed_two, wg_all)
    up_proj = add_rows(normed_two, wu_all)
    hidden = (jax.nn.silu(gate_proj) * up_proj).astype(jnp.bfloat16)
    down_terms = lax.dot_general(
        hidden, wd_t, (((1,), (1,)), ((), ())), preferred_element_type=jnp.float32
    )
    down_sum = swap_sum(down_terms.astype(jnp.bfloat16), "narrow")
    result = (first_res.astype(jnp.float32) + down_sum).astype(jnp.bfloat16)
    page_count = tok_rows // PAGE
    slots = page_table - wide_rank * page_count
    pairs = jnp.stack(
        [
            keys_rot.reshape(page_count, PAGE, local_width),
            values.reshape(page_count, PAGE, local_width),
        ],
        axis=0,
    )
    kv_cache = jnp.zeros_like(pairs).at[:, slots].set(pairs)
    return (result, kv_cache)


def solution(mesh):
    return jax.shard_map(
        per_device,
        mesh=mesh,
        in_specs=(
            P("wide", "narrow"),
            P("wide"),
            P("wide"),
            P("wide", "narrow"),
            P("wide", "narrow"),
            P("wide", "narrow"),
            P("narrow", "wide"),
            P("wide", "narrow"),
            P("wide", "narrow"),
            P("narrow", "wide"),
        ),
        out_specs=(P("wide", "narrow"), P(None, "wide", None, "narrow")),
        check_vma=False,
    )
```

```python
import jax
import jax.numpy as jnp
from jax import lax
from jax.sharding import PartitionSpec as P

HEAD_DIM = 128
REACH = 8
PAGE = 16


epsilon = 1e-05
rope_base = 10000.0


def shifted(value, axis, steps):
    count = lax.axis_size(axis)
    first, last = (max(0, -steps), min(count, count - steps))
    return lax.ppermute(value, axis, [(source, source + steps) for source in range(first, last)])


def swap_gather(value, axis):
    count = lax.axis_size(axis)
    rows, cols = value.shape
    copies = jnp.broadcast_to(value[None], (count, rows, cols))
    got = lax.all_to_all(copies, axis, 0, 0, tiled=True)
    return jnp.moveaxis(got, 0, 1).reshape(rows, cols * count)


def swap_sum(value, axis):
    count = lax.axis_size(axis)
    rows, width = value.shape
    cols = width // count
    pieces = jnp.moveaxis(value.reshape(rows, count, cols), 1, 0)
    got = lax.all_to_all(pieces, axis, 0, 0, tiled=True)
    return jnp.sum(got.astype(jnp.float32), axis=0)


def norm_rows(source):
    widened = source.astype(jnp.float32)
    center = widened - jnp.mean(widened, axis=-1, keepdims=True)
    spread = jnp.mean(center * center, axis=-1, keepdims=True)
    return (center * lax.rsqrt(spread + epsilon)).astype(jnp.bfloat16)


def rotate(projected, positions):
    head_size = projected.shape[-1]
    half_dim = head_size // 2
    frequency = jnp.power(rope_base, -jnp.arange(half_dim, dtype=jnp.float32) * 2.0 / head_size)
    angles = positions.astype(jnp.float32)[:, None] * frequency[None, :]
    cosine = jnp.cos(angles)[:, None, :]
    sine_part = jnp.sin(angles)[:, None, :]
    first_half = projected[..., :half_dim]
    second_half = projected[..., half_dim:]
    return jnp.concatenate(
        [
            first_half * cosine - second_half * sine_part,
            second_half * cosine + first_half * sine_part,
        ],
        axis=-1,
    )


def add_rows(source, piece):
    return jnp.dot(source, piece, preferred_element_type=jnp.float32)


def per_device(hidden_in, segment_ids, page_table, wq, wk, wv, wo, wg, wu, wd):
    tok_rows = hidden_in.shape[0]
    wide_rank = lax.axis_index("wide")
    local_index = jnp.arange(tok_rows, dtype=jnp.int32)

    attn_width = wq.shape[1]
    ff_width = wg.shape[1]
    pieces = [wq, wk, wv, wo.T, wg, wu, wd.T]
    widths = [piece.shape[1] for piece in pieces]
    gathered = lax.all_gather(jnp.concatenate(pieces, axis=1), "wide", axis=0, tiled=True)
    offsets = [sum(widths[:k]) for k in range(len(widths))]
    full = [gathered[:, o:o + w] for o, w in zip(offsets, widths)]
    wq_all, wk_all, wv_all, wo_t, wg_all, wu_all, wd_t = full

    id_blocks = []
    for step_back in range(REACH, 0, -1):
        got = shifted(segment_ids, "wide", step_back)
        id_blocks.append(jnp.where(wide_rank >= step_back, got, -1))
    id_blocks.append(segment_ids)
    window_ids = jnp.concatenate(id_blocks, axis=0)
    window_len = window_ids.shape[0]
    lead = REACH * tok_rows
    window_index = jnp.arange(window_len, dtype=jnp.int32)
    same = window_ids[None, :] == segment_ids[:, None]
    allowed = same & (window_index[None, :] <= lead + local_index[:, None])
    earlier = same & (window_index[None, :] < lead + local_index[:, None])
    positions = jnp.sum(earlier.astype(jnp.int32), axis=1)

    whole = swap_gather(hidden_in, "narrow")
    normed = norm_rows(whole)
    local_width = attn_width
    head_count = local_width // HEAD_DIM

    q_proj = add_rows(normed, wq_all)
    k_proj = add_rows(normed, wk_all)
    v_proj = add_rows(normed, wv_all)
    queries = rotate(q_proj.reshape(tok_rows, head_count, HEAD_DIM), positions).astype(jnp.bfloat16)
    keys_rot = rotate(k_proj.reshape(tok_rows, head_count, HEAD_DIM), positions).astype(
        jnp.bfloat16
    )
    values = v_proj.astype(jnp.bfloat16).reshape(tok_rows, head_count, HEAD_DIM)
    packed = jnp.concatenate([keys_rot, values], axis=2)
    far = shifted(packed, "wide", REACH)
    span = packed
    steps = 1
    while steps < REACH:
        span = jnp.concatenate([shifted(span, "wide", steps), span], axis=0)
        steps = steps * 2
    score_scale = HEAD_DIM ** (-0.5)
    kv_all = jnp.concatenate([far, span], axis=0)
    key_all = kv_all[:, :, :HEAD_DIM]
    value_all = kv_all[:, :, HEAD_DIM:]
    scores = (
        jnp.einsum("qhd,khd->hqk", queries, key_all, preferred_element_type=jnp.float32)
        * score_scale
    )
    scores = jnp.where(allowed[None], scores, -1e30)
    row_peak = jnp.max(scores, axis=-1, keepdims=True)
    exps = jnp.where(allowed[None], jnp.exp(scores - row_peak), 0.0)
    attn_probs = (exps / jnp.sum(exps, axis=-1, keepdims=True)).astype(jnp.bfloat16)
    mixed = jnp.einsum("hqk,khd->qhd", attn_probs, value_all, preferred_element_type=jnp.float32)
    attended = mixed.astype(jnp.bfloat16).reshape(tok_rows, local_width)
    attn_terms = lax.dot_general(
        attended, wo_t, (((1,), (1,)), ((), ())), preferred_element_type=jnp.float32
    )
    attn_sum = swap_sum(attn_terms.astype(jnp.bfloat16), "narrow")
    first_res = (hidden_in.astype(jnp.float32) + attn_sum).astype(jnp.bfloat16)
    whole_two = swap_gather(first_res, "narrow")
    normed_two = norm_rows(whole_two)

    gate_proj = add_rows(normed_two, wg_all)
    up_proj = add_rows(normed_two, wu_all)
    hidden = (jax.nn.silu(gate_proj) * up_proj).astype(jnp.bfloat16)
    down_terms = lax.dot_general(
        hidden, wd_t, (((1,), (1,)), ((), ())), preferred_element_type=jnp.float32
    )
    down_sum = swap_sum(down_terms.astype(jnp.bfloat16), "narrow")
    result = (first_res.astype(jnp.float32) + down_sum).astype(jnp.bfloat16)
    page_count = tok_rows // PAGE
    slots = page_table - wide_rank * page_count
    pairs = jnp.stack(
        [
            keys_rot.reshape(page_count, PAGE, local_width),
            values.reshape(page_count, PAGE, local_width),
        ],
        axis=0,
    )
    kv_cache = jnp.zeros_like(pairs).at[:, slots].set(pairs)
    return (result, kv_cache)


def solution(mesh):
    return jax.shard_map(
        per_device,
        mesh=mesh,
        in_specs=(
            P("wide", "narrow"),
            P("wide"),
            P("wide"),
            P("wide", "narrow"),
            P("wide", "narrow"),
            P("wide", "narrow"),
            P("narrow", "wide"),
            P("wide", "narrow"),
            P("wide", "narrow"),
            P("narrow", "wide"),
        ),
        out_specs=(P("wide", "narrow"), P(None, "wide", None, "narrow")),
        check_vma=False,
    )
```

```python
import jax
import jax.numpy as jnp
from jax import lax
from jax.sharding import PartitionSpec as P

HEAD_DIM = 128
REACH = 8
PAGE = 16


epsilon = 1e-05
rope_base = 10000.0


def shifted(value, axis, steps):
    count = lax.axis_size(axis)
    first, last = (max(0, -steps), min(count, count - steps))
    return lax.ppermute(value, axis, [(source, source + steps) for source in range(first, last)])


def swap_gather(value, axis):
    count = lax.axis_size(axis)
    rows, cols = value.shape
    copies = jnp.broadcast_to(value[None], (count, rows, cols))
    got = lax.all_to_all(copies, axis, 0, 0, tiled=True)
    return jnp.moveaxis(got, 0, 1).reshape(rows, cols * count)


def swap_sum(value, axis):
    count = lax.axis_size(axis)
    rows, width = value.shape
    cols = width // count
    pieces = jnp.moveaxis(value.reshape(rows, count, cols), 1, 0)
    got = lax.all_to_all(pieces, axis, 0, 0, tiled=True)
    return jnp.sum(got.astype(jnp.float32), axis=0)


def norm_rows(source):
    widened = source.astype(jnp.float32)
    center = widened - jnp.mean(widened, axis=-1, keepdims=True)
    spread = jnp.mean(center * center, axis=-1, keepdims=True)
    return (center * lax.rsqrt(spread + epsilon)).astype(jnp.bfloat16)


def rotate(projected, positions):
    head_size = projected.shape[-1]
    half_dim = head_size // 2
    frequency = jnp.power(rope_base, -jnp.arange(half_dim, dtype=jnp.float32) * 2.0 / head_size)
    angles = positions.astype(jnp.float32)[:, None] * frequency[None, :]
    cosine = jnp.cos(angles)[:, None, :]
    sine_part = jnp.sin(angles)[:, None, :]
    first_half = projected[..., :half_dim]
    second_half = projected[..., half_dim:]
    return jnp.concatenate(
        [
            first_half * cosine - second_half * sine_part,
            second_half * cosine + first_half * sine_part,
        ],
        axis=-1,
    )


def add_rows(source, piece):
    return jnp.dot(source, piece, preferred_element_type=jnp.float32)


def per_device(hidden_in, segment_ids, page_table, wq, wk, wv, wo, wg, wu, wd):
    tok_rows = hidden_in.shape[0]
    wide_rank = lax.axis_index("wide")
    local_index = jnp.arange(tok_rows, dtype=jnp.int32)

    attn_width = wq.shape[1]
    pieces = [wq, wo.T, wg, wu, wd.T]
    widths = [piece.shape[1] for piece in pieces]
    gathered = lax.all_gather(jnp.concatenate(pieces, axis=1), "wide", axis=0, tiled=True)
    offsets = [sum(widths[:k]) for k in range(len(widths))]
    wq_all, wo_t, wg_all, wu_all, wd_t = [gathered[:, o:o + w] for o, w in zip(offsets, widths)]

    count = lax.axis_size("wide")
    rows = wk.shape[0]
    id_rows = segment_ids.astype(jnp.bfloat16).reshape(rows, tok_rows // rows)
    early = jnp.concatenate([wk, wv, id_rows], axis=1)
    early_all = lax.all_to_all(
        jnp.broadcast_to(early[None], (count,) + early.shape), "wide", 0, 0, tiled=True
    ).reshape(count * rows, early.shape[1])
    wk_all = early_all[:, :attn_width]
    wv_all = early_all[:, attn_width:2 * attn_width]
    all_ids = early_all[:, 2 * attn_width:].reshape(-1).astype(jnp.int32)

    lead = REACH * tok_rows
    padded_ids = jnp.concatenate([jnp.full((lead,), -1, jnp.int32), all_ids], axis=0)
    window_ids = lax.dynamic_slice_in_dim(padded_ids, wide_rank * tok_rows, lead + tok_rows)
    window_len = window_ids.shape[0]
    window_index = jnp.arange(window_len, dtype=jnp.int32)
    same = window_ids[None, :] == segment_ids[:, None]
    allowed = same & (window_index[None, :] <= lead + local_index[:, None])
    earlier = same & (window_index[None, :] < lead + local_index[:, None])
    positions = jnp.sum(earlier.astype(jnp.int32), axis=1)

    whole = swap_gather(hidden_in, "narrow")
    normed = norm_rows(whole)
    local_width = attn_width
    head_count = local_width // HEAD_DIM

    q_proj = add_rows(normed, wq_all)
    k_proj = add_rows(normed, wk_all)
    v_proj = add_rows(normed, wv_all)
    queries = rotate(q_proj.reshape(tok_rows, head_count, HEAD_DIM), positions).astype(jnp.bfloat16)
    keys_rot = rotate(k_proj.reshape(tok_rows, head_count, HEAD_DIM), positions).astype(
        jnp.bfloat16
    )
    values = v_proj.astype(jnp.bfloat16).reshape(tok_rows, head_count, HEAD_DIM)
    packed = jnp.concatenate([keys_rot, values], axis=2)
    far = shifted(packed, "wide", REACH)
    span = packed
    steps = 1
    while steps < REACH:
        span = jnp.concatenate([shifted(span, "wide", steps), span], axis=0)
        steps = steps * 2
    score_scale = HEAD_DIM ** (-0.5)
    kv_all = jnp.concatenate([far, span], axis=0)
    key_all = kv_all[:, :, :HEAD_DIM]
    value_all = kv_all[:, :, HEAD_DIM:]
    scores = (
        jnp.einsum("qhd,khd->hqk", queries, key_all, preferred_element_type=jnp.float32)
        * score_scale
    )
    scores = jnp.where(allowed[None], scores, -1e30)
    row_peak = jnp.max(scores, axis=-1, keepdims=True)
    exps = jnp.where(allowed[None], jnp.exp(scores - row_peak), 0.0)
    attn_probs = (exps / jnp.sum(exps, axis=-1, keepdims=True)).astype(jnp.bfloat16)
    mixed = jnp.einsum("hqk,khd->qhd", attn_probs, value_all, preferred_element_type=jnp.float32)
    attended = mixed.astype(jnp.bfloat16).reshape(tok_rows, local_width)
    attn_terms = lax.dot_general(
        attended, wo_t, (((1,), (1,)), ((), ())), preferred_element_type=jnp.float32
    )
    attn_sum = swap_sum(attn_terms.astype(jnp.bfloat16), "narrow")
    first_res = (hidden_in.astype(jnp.float32) + attn_sum).astype(jnp.bfloat16)
    whole_two = swap_gather(first_res, "narrow")
    normed_two = norm_rows(whole_two)

    gate_proj = add_rows(normed_two, wg_all)
    up_proj = add_rows(normed_two, wu_all)
    hidden = (jax.nn.silu(gate_proj) * up_proj).astype(jnp.bfloat16)
    down_terms = lax.dot_general(
        hidden, wd_t, (((1,), (1,)), ((), ())), preferred_element_type=jnp.float32
    )
    down_sum = swap_sum(down_terms.astype(jnp.bfloat16), "narrow")
    result = (first_res.astype(jnp.float32) + down_sum).astype(jnp.bfloat16)
    page_count = tok_rows // PAGE
    slots = page_table - wide_rank * page_count
    pairs = jnp.stack(
        [
            keys_rot.reshape(page_count, PAGE, local_width),
            values.reshape(page_count, PAGE, local_width),
        ],
        axis=0,
    )
    kv_cache = jnp.zeros_like(pairs).at[:, slots].set(pairs)
    return (result, kv_cache)


def solution(mesh):
    return jax.shard_map(
        per_device,
        mesh=mesh,
        in_specs=(
            P("wide", "narrow"),
            P("wide"),
            P("wide"),
            P("wide", "narrow"),
            P("wide", "narrow"),
            P("wide", "narrow"),
            P("narrow", "wide"),
            P("wide", "narrow"),
            P("wide", "narrow"),
            P("narrow", "wide"),
        ),
        out_specs=(P("wide", "narrow"), P(None, "wide", None, "narrow")),
        check_vma=False,
    )
```

```python
import jax
import jax.numpy as jnp
from jax import lax
from jax.sharding import PartitionSpec as P

HEAD_DIM = 128
REACH = 8
PAGE = 16


epsilon = 1e-05
rope_base = 10000.0


def shifted(value, axis, steps):
    count = lax.axis_size(axis)
    first, last = (max(0, -steps), min(count, count - steps))
    return lax.ppermute(value, axis, [(source, source + steps) for source in range(first, last)])


def swap_gather(value, axis):
    count = lax.axis_size(axis)
    rows, cols = value.shape
    copies = jnp.broadcast_to(value[None], (count, rows, cols))
    got = lax.all_to_all(copies, axis, 0, 0, tiled=True)
    return jnp.moveaxis(got, 0, 1).reshape(rows, cols * count)


def swap_sum(value, axis):
    count = lax.axis_size(axis)
    rows, width = value.shape
    cols = width // count
    pieces = jnp.moveaxis(value.reshape(rows, count, cols), 1, 0)
    got = lax.all_to_all(pieces, axis, 0, 0, tiled=True)
    return jnp.sum(got.astype(jnp.float32), axis=0)


def norm_rows(source):
    widened = source.astype(jnp.float32)
    center = widened - jnp.mean(widened, axis=-1, keepdims=True)
    spread = jnp.mean(center * center, axis=-1, keepdims=True)
    return (center * lax.rsqrt(spread + epsilon)).astype(jnp.bfloat16)


def rotate(projected, positions):
    head_size = projected.shape[-1]
    half_dim = head_size // 2
    frequency = jnp.power(rope_base, -jnp.arange(half_dim, dtype=jnp.float32) * 2.0 / head_size)
    angles = positions.astype(jnp.float32)[:, None] * frequency[None, :]
    cosine = jnp.cos(angles)[:, None, :]
    sine_part = jnp.sin(angles)[:, None, :]
    first_half = projected[..., :half_dim]
    second_half = projected[..., half_dim:]
    return jnp.concatenate(
        [
            first_half * cosine - second_half * sine_part,
            second_half * cosine + first_half * sine_part,
        ],
        axis=-1,
    )


def add_rows(source, piece):
    return jnp.dot(source, piece, preferred_element_type=jnp.float32)


def per_device(hidden_in, segment_ids, page_table, wq, wk, wv, wo, wg, wu, wd):
    tok_rows = hidden_in.shape[0]
    wide_rank = lax.axis_index("wide")
    local_index = jnp.arange(tok_rows, dtype=jnp.int32)

    attn_width = wq.shape[1]
    ff_width = wg.shape[1]
    pieces = [wq, wk, wv, wo.T, wg, wu, wd.T]
    widths = [piece.shape[1] for piece in pieces]
    gathered = lax.all_gather(jnp.concatenate(pieces, axis=1), "wide", axis=0, tiled=True)
    offsets = [sum(widths[:k]) for k in range(len(widths))]
    full = [gathered[:, o:o + w] for o, w in zip(offsets, widths)]
    wq_all, wk_all, wv_all, wo_t, wg_all, wu_all, wd_t = full

    id_blocks = []
    for step_back in range(REACH, 0, -1):
        got = shifted(segment_ids, "wide", step_back)
        id_blocks.append(jnp.where(wide_rank >= step_back, got, -1))
    id_blocks.append(segment_ids)
    window_ids = jnp.concatenate(id_blocks, axis=0)
    window_len = window_ids.shape[0]
    lead = REACH * tok_rows
    window_index = jnp.arange(window_len, dtype=jnp.int32)
    same = window_ids[None, :] == segment_ids[:, None]
    earlier = same & (window_index[None, :] < lead + local_index[:, None])
    positions = jnp.sum(earlier.astype(jnp.int32), axis=1)

    whole = swap_gather(hidden_in, "narrow")
    normed = norm_rows(whole)
    local_width = attn_width
    head_count = local_width // HEAD_DIM

    q_proj = add_rows(normed, wq_all)
    k_proj = add_rows(normed, wk_all)
    v_proj = add_rows(normed, wv_all)
    queries = rotate(q_proj.reshape(tok_rows, head_count, HEAD_DIM), positions).astype(jnp.bfloat16)
    keys_rot = rotate(k_proj.reshape(tok_rows, head_count, HEAD_DIM), positions).astype(
        jnp.bfloat16
    )
    values = v_proj.astype(jnp.bfloat16).reshape(tok_rows, head_count, HEAD_DIM)
    packed = jnp.concatenate([keys_rot, values], axis=2)
    pairs_per_chip = 2
    chips_back = REACH // pairs_per_chip
    line = [shifted(packed, "wide", pairs_per_chip * step) for step in range(1, chips_back + 1)]
    count = lax.axis_size("wide")
    partner = lax.ppermute(
        jnp.stack(line + [packed], axis=0), "wide", [(i, i ^ 1) for i in range(count)]
    )
    partner_rank = wide_rank ^ 1
    order = []
    block_ids = []
    for step in range(chips_back, 0, -1):
        order += [line[step - 1], partner[step - 1]]
        block_ids += [wide_rank - pairs_per_chip * step, partner_rank - pairs_per_chip * step]
    order += [partner[chips_back], packed]
    block_ids += [partner_rank, wide_rank]
    kv_all = jnp.concatenate(order, axis=0)
    key_index = (
        jnp.stack(block_ids)[:, None] * tok_rows + local_index[None, :]
    ).reshape(-1)
    query_index = wide_rank * tok_rows + local_index
    query_start = query_index - positions
    allowed = (key_index[None, :] >= query_start[:, None]) & (key_index[None, :] <= query_index[:, None])
    score_scale = HEAD_DIM ** (-0.5)
    key_all = kv_all[:, :, :HEAD_DIM]
    value_all = kv_all[:, :, HEAD_DIM:]
    scores = (
        jnp.einsum("qhd,khd->hqk", queries, key_all, preferred_element_type=jnp.float32)
        * score_scale
    )
    scores = jnp.where(allowed[None], scores, -1e30)
    row_peak = jnp.max(scores, axis=-1, keepdims=True)
    exps = jnp.where(allowed[None], jnp.exp(scores - row_peak), 0.0)
    attn_probs = (exps / jnp.sum(exps, axis=-1, keepdims=True)).astype(jnp.bfloat16)
    mixed = jnp.einsum("hqk,khd->qhd", attn_probs, value_all, preferred_element_type=jnp.float32)
    attended = mixed.astype(jnp.bfloat16).reshape(tok_rows, local_width)
    attn_terms = lax.dot_general(
        attended, wo_t, (((1,), (1,)), ((), ())), preferred_element_type=jnp.float32
    )
    attn_sum = swap_sum(attn_terms.astype(jnp.bfloat16), "narrow")
    first_res = (hidden_in.astype(jnp.float32) + attn_sum).astype(jnp.bfloat16)
    whole_two = swap_gather(first_res, "narrow")
    normed_two = norm_rows(whole_two)

    gate_proj = add_rows(normed_two, wg_all)
    up_proj = add_rows(normed_two, wu_all)
    hidden = (jax.nn.silu(gate_proj) * up_proj).astype(jnp.bfloat16)
    down_terms = lax.dot_general(
        hidden, wd_t, (((1,), (1,)), ((), ())), preferred_element_type=jnp.float32
    )
    down_sum = swap_sum(down_terms.astype(jnp.bfloat16), "narrow")
    result = (first_res.astype(jnp.float32) + down_sum).astype(jnp.bfloat16)
    page_count = tok_rows // PAGE
    slots = page_table - wide_rank * page_count
    pairs = jnp.stack(
        [
            keys_rot.reshape(page_count, PAGE, local_width),
            values.reshape(page_count, PAGE, local_width),
        ],
        axis=0,
    )
    kv_cache = jnp.zeros_like(pairs).at[:, slots].set(pairs)
    return (result, kv_cache)


def solution(mesh):
    return jax.shard_map(
        per_device,
        mesh=mesh,
        in_specs=(
            P("wide", "narrow"),
            P("wide"),
            P("wide"),
            P("wide", "narrow"),
            P("wide", "narrow"),
            P("wide", "narrow"),
            P("narrow", "wide"),
            P("wide", "narrow"),
            P("wide", "narrow"),
            P("narrow", "wide"),
        ),
        out_specs=(P("wide", "narrow"), P(None, "wide", None, "narrow")),
        check_vma=False,
    )
```

```python
import jax
import jax.numpy as jnp
from jax import lax
from jax.sharding import PartitionSpec as P

HEAD_DIM = 128
REACH = 8
PAGE = 16


epsilon = 1e-05
rope_base = 10000.0


def shifted(value, axis, steps):
    count = lax.axis_size(axis)
    first, last = (max(0, -steps), min(count, count - steps))
    return lax.ppermute(value, axis, [(source, source + steps) for source in range(first, last)])


def swap_gather(value, axis):
    count = lax.axis_size(axis)
    rows, cols = value.shape
    copies = jnp.broadcast_to(value[None], (count, rows, cols))
    got = lax.all_to_all(copies, axis, 0, 0, tiled=True)
    return jnp.moveaxis(got, 0, 1).reshape(rows, cols * count)


def swap_sum(value, axis):
    count = lax.axis_size(axis)
    rows, width = value.shape
    cols = width // count
    pieces = jnp.moveaxis(value.reshape(rows, count, cols), 1, 0)
    got = lax.all_to_all(pieces, axis, 0, 0, tiled=True)
    return jnp.sum(got.astype(jnp.float32), axis=0)


def norm_rows(source):
    widened = source.astype(jnp.float32)
    center = widened - jnp.mean(widened, axis=-1, keepdims=True)
    spread = jnp.mean(center * center, axis=-1, keepdims=True)
    return (center * lax.rsqrt(spread + epsilon)).astype(jnp.bfloat16)


def rotate(projected, positions):
    head_size = projected.shape[-1]
    half_dim = head_size // 2
    frequency = jnp.power(rope_base, -jnp.arange(half_dim, dtype=jnp.float32) * 2.0 / head_size)
    angles = positions.astype(jnp.float32)[:, None] * frequency[None, :]
    cosine = jnp.cos(angles)[:, None, :]
    sine_part = jnp.sin(angles)[:, None, :]
    first_half = projected[..., :half_dim]
    second_half = projected[..., half_dim:]
    return jnp.concatenate(
        [
            first_half * cosine - second_half * sine_part,
            second_half * cosine + first_half * sine_part,
        ],
        axis=-1,
    )


def add_rows(source, piece):
    return jnp.dot(source, piece, preferred_element_type=jnp.float32)


def per_device(hidden_in, segment_ids, page_table, wq, wk, wv, wo, wg, wu, wd):
    tok_rows = hidden_in.shape[0]
    wide_rank = lax.axis_index("wide")
    local_index = jnp.arange(tok_rows, dtype=jnp.int32)

    attn_width = wq.shape[1]

    def gather_pieces(pieces):
        widths = [piece.shape[1] for piece in pieces]
        gathered = lax.all_gather(jnp.concatenate(pieces, axis=1), "wide", axis=0, tiled=True)
        offsets = [sum(widths[:k]) for k in range(len(widths))]
        return [gathered[:, o:o + w] for o, w in zip(offsets, widths)]

    wq_all, wk_all, wv_all, wo_t = gather_pieces([wq, wk, wv, wo.T])
    wg_all, wu_all, wd_t = gather_pieces([wg, wu, wd.T])

    id_blocks = []
    for step_back in range(REACH, 0, -1):
        got = shifted(segment_ids, "wide", step_back)
        id_blocks.append(jnp.where(wide_rank >= step_back, got, -1))
    id_blocks.append(segment_ids)
    window_ids = jnp.concatenate(id_blocks, axis=0)
    window_len = window_ids.shape[0]
    lead = REACH * tok_rows
    window_index = jnp.arange(window_len, dtype=jnp.int32)
    same = window_ids[None, :] == segment_ids[:, None]
    earlier = same & (window_index[None, :] < lead + local_index[:, None])
    positions = jnp.sum(earlier.astype(jnp.int32), axis=1)

    whole = swap_gather(hidden_in, "narrow")
    normed = norm_rows(whole)
    local_width = attn_width
    head_count = local_width // HEAD_DIM

    q_proj = add_rows(normed, wq_all)
    k_proj = add_rows(normed, wk_all)
    v_proj = add_rows(normed, wv_all)
    queries = rotate(q_proj.reshape(tok_rows, head_count, HEAD_DIM), positions).astype(jnp.bfloat16)
    keys_rot = rotate(k_proj.reshape(tok_rows, head_count, HEAD_DIM), positions).astype(
        jnp.bfloat16
    )
    values = v_proj.astype(jnp.bfloat16).reshape(tok_rows, head_count, HEAD_DIM)
    packed = jnp.concatenate([keys_rot, values], axis=2)
    pairs_per_chip = 2
    chips_back = REACH // pairs_per_chip
    line = [shifted(packed, "wide", pairs_per_chip * step) for step in range(1, chips_back + 1)]
    count = lax.axis_size("wide")
    partner = lax.ppermute(
        jnp.stack(line + [packed], axis=0), "wide", [(i, i ^ 1) for i in range(count)]
    )
    partner_rank = wide_rank ^ 1
    order = []
    block_ids = []
    for step in range(chips_back, 0, -1):
        order += [line[step - 1], partner[step - 1]]
        block_ids += [wide_rank - pairs_per_chip * step, partner_rank - pairs_per_chip * step]
    order += [partner[chips_back], packed]
    block_ids += [partner_rank, wide_rank]
    kv_all = jnp.concatenate(order, axis=0)
    key_index = (
        jnp.stack(block_ids)[:, None] * tok_rows + local_index[None, :]
    ).reshape(-1)
    query_index = wide_rank * tok_rows + local_index
    query_start = query_index - positions
    allowed = (key_index[None, :] >= query_start[:, None]) & (key_index[None, :] <= query_index[:, None])
    score_scale = HEAD_DIM ** (-0.5)
    key_all = kv_all[:, :, :HEAD_DIM]
    value_all = kv_all[:, :, HEAD_DIM:]
    scores = (
        jnp.einsum("qhd,khd->hqk", queries, key_all, preferred_element_type=jnp.float32)
        * score_scale
    )
    scores = jnp.where(allowed[None], scores, -1e30)
    row_peak = jnp.max(scores, axis=-1, keepdims=True)
    exps = jnp.where(allowed[None], jnp.exp(scores - row_peak), 0.0)
    attn_probs = (exps / jnp.sum(exps, axis=-1, keepdims=True)).astype(jnp.bfloat16)
    mixed = jnp.einsum("hqk,khd->qhd", attn_probs, value_all, preferred_element_type=jnp.float32)
    attended = mixed.astype(jnp.bfloat16).reshape(tok_rows, local_width)
    attn_terms = lax.dot_general(
        attended, wo_t, (((1,), (1,)), ((), ())), preferred_element_type=jnp.float32
    )
    attn_sum = swap_sum(attn_terms.astype(jnp.bfloat16), "narrow")
    first_res = (hidden_in.astype(jnp.float32) + attn_sum).astype(jnp.bfloat16)
    whole_two = swap_gather(first_res, "narrow")
    normed_two = norm_rows(whole_two)

    gate_proj = add_rows(normed_two, wg_all)
    up_proj = add_rows(normed_two, wu_all)
    hidden = (jax.nn.silu(gate_proj) * up_proj).astype(jnp.bfloat16)
    down_terms = lax.dot_general(
        hidden, wd_t, (((1,), (1,)), ((), ())), preferred_element_type=jnp.float32
    )
    down_sum = swap_sum(down_terms.astype(jnp.bfloat16), "narrow")
    result = (first_res.astype(jnp.float32) + down_sum).astype(jnp.bfloat16)
    page_count = tok_rows // PAGE
    slots = page_table - wide_rank * page_count
    pairs = jnp.stack(
        [
            keys_rot.reshape(page_count, PAGE, local_width),
            values.reshape(page_count, PAGE, local_width),
        ],
        axis=0,
    )
    kv_cache = jnp.zeros_like(pairs).at[:, slots].set(pairs)
    return (result, kv_cache)


def solution(mesh):
    return jax.shard_map(
        per_device,
        mesh=mesh,
        in_specs=(
            P("wide", "narrow"),
            P("wide"),
            P("wide"),
            P("wide", "narrow"),
            P("wide", "narrow"),
            P("wide", "narrow"),
            P("narrow", "wide"),
            P("wide", "narrow"),
            P("wide", "narrow"),
            P("narrow", "wide"),
        ),
        out_specs=(P("wide", "narrow"), P(None, "wide", None, "narrow")),
        check_vma=False,
    )
```

```python
import jax
import jax.numpy as jnp
from jax import lax
from jax.sharding import PartitionSpec as P

HEAD_DIM = 128
REACH = 8
PAGE = 16


epsilon = 1e-05
rope_base = 10000.0


def shifted(value, axis, steps):
    count = lax.axis_size(axis)
    first, last = (max(0, -steps), min(count, count - steps))
    return lax.ppermute(value, axis, [(source, source + steps) for source in range(first, last)])


def swap_gather(value, axis):
    count = lax.axis_size(axis)
    rows, cols = value.shape
    copies = jnp.broadcast_to(value[None], (count, rows, cols))
    got = lax.all_to_all(copies, axis, 0, 0, tiled=True)
    return jnp.moveaxis(got, 0, 1).reshape(rows, cols * count)


def swap_sum(value, axis):
    count = lax.axis_size(axis)
    rows, width = value.shape
    cols = width // count
    pieces = jnp.moveaxis(value.reshape(rows, count, cols), 1, 0)
    got = lax.all_to_all(pieces, axis, 0, 0, tiled=True)
    return jnp.sum(got.astype(jnp.float32), axis=0)


def norm_rows(source):
    widened = source.astype(jnp.float32)
    center = widened - jnp.mean(widened, axis=-1, keepdims=True)
    spread = jnp.mean(center * center, axis=-1, keepdims=True)
    return (center * lax.rsqrt(spread + epsilon)).astype(jnp.bfloat16)


def rotate(projected, positions):
    head_size = projected.shape[-1]
    half_dim = head_size // 2
    frequency = jnp.power(rope_base, -jnp.arange(half_dim, dtype=jnp.float32) * 2.0 / head_size)
    angles = positions.astype(jnp.float32)[:, None] * frequency[None, :]
    cosine = jnp.cos(angles)[:, None, :]
    sine_part = jnp.sin(angles)[:, None, :]
    first_half = projected[..., :half_dim]
    second_half = projected[..., half_dim:]
    return jnp.concatenate(
        [
            first_half * cosine - second_half * sine_part,
            second_half * cosine + first_half * sine_part,
        ],
        axis=-1,
    )


def add_rows(source, piece):
    return jnp.dot(source, piece, preferred_element_type=jnp.float32)


def per_device(hidden_in, segment_ids, page_table, wq, wk, wv, wo, wg, wu, wd):
    tok_rows = hidden_in.shape[0]
    wide_rank = lax.axis_index("wide")
    local_index = jnp.arange(tok_rows, dtype=jnp.int32)

    attn_width = wq.shape[1]

    def gather_pieces(pieces):
        widths = [piece.shape[1] for piece in pieces]
        gathered = lax.all_gather(jnp.concatenate(pieces, axis=1), "wide", axis=0, tiled=True)
        offsets = [sum(widths[:k]) for k in range(len(widths))]
        return [gathered[:, o:o + w] for o, w in zip(offsets, widths)]

    attn_pieces = [wq, wk, wv, wo.T]
    attn_gathered = lax.all_gather(jnp.concatenate(attn_pieces, axis=1), "wide", axis=0, tiled=True)
    wo_t = attn_gathered[:, 3 * attn_width:]
    wg_all, wu_all, wd_t = gather_pieces([wg, wu, wd.T])

    id_blocks = []
    for step_back in range(REACH, 0, -1):
        got = shifted(segment_ids, "wide", step_back)
        id_blocks.append(jnp.where(wide_rank >= step_back, got, -1))
    id_blocks.append(segment_ids)
    window_ids = jnp.concatenate(id_blocks, axis=0)
    window_len = window_ids.shape[0]
    lead = REACH * tok_rows
    window_index = jnp.arange(window_len, dtype=jnp.int32)
    same = window_ids[None, :] == segment_ids[:, None]
    earlier = same & (window_index[None, :] < lead + local_index[:, None])
    positions = jnp.sum(earlier.astype(jnp.int32), axis=1)

    whole = swap_gather(hidden_in, "narrow")
    normed = norm_rows(whole)
    local_width = attn_width
    head_count = local_width // HEAD_DIM

    projected = add_rows(normed, attn_gathered)
    q_proj = projected[:, :attn_width]
    k_proj = projected[:, attn_width:2 * attn_width]
    v_proj = projected[:, 2 * attn_width:3 * attn_width]
    queries = rotate(q_proj.reshape(tok_rows, head_count, HEAD_DIM), positions).astype(jnp.bfloat16)
    keys_rot = rotate(k_proj.reshape(tok_rows, head_count, HEAD_DIM), positions).astype(
        jnp.bfloat16
    )
    values = v_proj.astype(jnp.bfloat16).reshape(tok_rows, head_count, HEAD_DIM)
    packed = jnp.concatenate([keys_rot, values], axis=2)
    pairs_per_chip = 2
    chips_back = REACH // pairs_per_chip
    line = [shifted(packed, "wide", pairs_per_chip * step) for step in range(1, chips_back + 1)]
    count = lax.axis_size("wide")
    partner = lax.ppermute(
        jnp.stack(line + [packed], axis=0), "wide", [(i, i ^ 1) for i in range(count)]
    )
    partner_rank = wide_rank ^ 1
    order = []
    block_ids = []
    for step in range(chips_back, 0, -1):
        order += [line[step - 1], partner[step - 1]]
        block_ids += [wide_rank - pairs_per_chip * step, partner_rank - pairs_per_chip * step]
    order += [partner[chips_back], packed]
    block_ids += [partner_rank, wide_rank]
    kv_all = jnp.concatenate(order, axis=0)
    key_index = (
        jnp.stack(block_ids)[:, None] * tok_rows + local_index[None, :]
    ).reshape(-1)
    query_index = wide_rank * tok_rows + local_index
    query_start = query_index - positions
    allowed = (key_index[None, :] >= query_start[:, None]) & (key_index[None, :] <= query_index[:, None])
    score_scale = HEAD_DIM ** (-0.5)
    key_all = kv_all[:, :, :HEAD_DIM]
    value_all = kv_all[:, :, HEAD_DIM:]
    scores = (
        jnp.einsum("qhd,khd->hqk", queries, key_all, preferred_element_type=jnp.float32)
        * score_scale
    )
    scores = jnp.where(allowed[None], scores, -1e30)
    row_peak = jnp.max(scores, axis=-1, keepdims=True)
    exps = jnp.where(allowed[None], jnp.exp(scores - row_peak), 0.0)
    attn_probs = (exps / jnp.sum(exps, axis=-1, keepdims=True)).astype(jnp.bfloat16)
    mixed = jnp.einsum("hqk,khd->qhd", attn_probs, value_all, preferred_element_type=jnp.float32)
    attended = mixed.astype(jnp.bfloat16).reshape(tok_rows, local_width)
    attn_terms = lax.dot_general(
        attended, wo_t, (((1,), (1,)), ((), ())), preferred_element_type=jnp.float32
    )
    attn_sum = swap_sum(attn_terms.astype(jnp.bfloat16), "narrow")
    first_res = (hidden_in.astype(jnp.float32) + attn_sum).astype(jnp.bfloat16)
    whole_two = swap_gather(first_res, "narrow")
    normed_two = norm_rows(whole_two)

    gate_proj = add_rows(normed_two, wg_all)
    up_proj = add_rows(normed_two, wu_all)
    hidden = (jax.nn.silu(gate_proj) * up_proj).astype(jnp.bfloat16)
    down_terms = lax.dot_general(
        hidden, wd_t, (((1,), (1,)), ((), ())), preferred_element_type=jnp.float32
    )
    down_sum = swap_sum(down_terms.astype(jnp.bfloat16), "narrow")
    result = (first_res.astype(jnp.float32) + down_sum).astype(jnp.bfloat16)
    page_count = tok_rows // PAGE
    slots = page_table - wide_rank * page_count
    pairs = jnp.stack(
        [
            keys_rot.reshape(page_count, PAGE, local_width),
            values.reshape(page_count, PAGE, local_width),
        ],
        axis=0,
    )
    kv_cache = jnp.zeros_like(pairs).at[:, slots].set(pairs)
    return (result, kv_cache)


def solution(mesh):
    return jax.shard_map(
        per_device,
        mesh=mesh,
        in_specs=(
            P("wide", "narrow"),
            P("wide"),
            P("wide"),
            P("wide", "narrow"),
            P("wide", "narrow"),
            P("wide", "narrow"),
            P("narrow", "wide"),
            P("wide", "narrow"),
            P("wide", "narrow"),
            P("narrow", "wide"),
        ),
        out_specs=(P("wide", "narrow"), P(None, "wide", None, "narrow")),
        check_vma=False,
    )
```

```python
import jax
import jax.numpy as jnp
from jax import lax
from jax.sharding import PartitionSpec as P

HEAD_DIM = 128
REACH = 8
PAGE = 16


epsilon = 1e-05
rope_base = 10000.0


def shifted(value, axis, steps):
    count = lax.axis_size(axis)
    first, last = (max(0, -steps), min(count, count - steps))
    return lax.ppermute(value, axis, [(source, source + steps) for source in range(first, last)])


def swap_gather(value, axis):
    count = lax.axis_size(axis)
    rows, cols = value.shape
    copies = jnp.broadcast_to(value[None], (count, rows, cols))
    got = lax.all_to_all(copies, axis, 0, 0, tiled=True)
    return jnp.moveaxis(got, 0, 1).reshape(rows, cols * count)


def swap_sum(value, axis):
    count = lax.axis_size(axis)
    rows, width = value.shape
    cols = width // count
    pieces = jnp.moveaxis(value.reshape(rows, count, cols), 1, 0)
    got = lax.all_to_all(pieces, axis, 0, 0, tiled=True)
    return jnp.sum(got.astype(jnp.float32), axis=0)


def norm_rows(source):
    widened = source.astype(jnp.float32)
    center = widened - jnp.mean(widened, axis=-1, keepdims=True)
    spread = jnp.mean(center * center, axis=-1, keepdims=True)
    return (center * lax.rsqrt(spread + epsilon)).astype(jnp.bfloat16)


def rotate(projected, positions):
    head_size = projected.shape[-1]
    half_dim = head_size // 2
    frequency = jnp.power(rope_base, -jnp.arange(half_dim, dtype=jnp.float32) * 2.0 / head_size)
    angles = positions.astype(jnp.float32)[:, None] * frequency[None, :]
    cosine = jnp.cos(angles)[:, None, :]
    sine_part = jnp.sin(angles)[:, None, :]
    first_half = projected[..., :half_dim]
    second_half = projected[..., half_dim:]
    return jnp.concatenate(
        [
            first_half * cosine - second_half * sine_part,
            second_half * cosine + first_half * sine_part,
        ],
        axis=-1,
    )


def add_rows(source, piece):
    return jnp.dot(source, piece, preferred_element_type=jnp.float32)


def per_device(hidden_in, segment_ids, page_table, wq, wk, wv, wo, wg, wu, wd):
    tok_rows = hidden_in.shape[0]
    wide_rank = lax.axis_index("wide")
    local_index = jnp.arange(tok_rows, dtype=jnp.int32)

    attn_width = wq.shape[1]

    def gather_pieces(pieces):
        widths = [piece.shape[1] for piece in pieces]
        gathered = lax.all_gather(jnp.concatenate(pieces, axis=1), "wide", axis=0, tiled=True)
        offsets = [sum(widths[:k]) for k in range(len(widths))]
        return [gathered[:, o:o + w] for o, w in zip(offsets, widths)]

    attn_pieces = [wq, wk, wv, wo.T]
    attn_gathered = lax.all_gather(jnp.concatenate(attn_pieces, axis=1), "wide", axis=0, tiled=True)
    wo_t = attn_gathered[:, 3 * attn_width:]
    wg_all, wu_all, wd_t = gather_pieces([wg, wu, wd.T])

    id_blocks = []
    for step_back in range(REACH, 0, -1):
        got = shifted(segment_ids, "wide", step_back)
        id_blocks.append(jnp.where(wide_rank >= step_back, got, -1))
    id_blocks.append(segment_ids)
    window_ids = jnp.concatenate(id_blocks, axis=0)
    window_len = window_ids.shape[0]
    lead = REACH * tok_rows
    window_index = jnp.arange(window_len, dtype=jnp.int32)
    same = window_ids[None, :] == segment_ids[:, None]
    earlier = same & (window_index[None, :] < lead + local_index[:, None])
    positions = jnp.sum(earlier.astype(jnp.int32), axis=1)

    whole = swap_gather(hidden_in, "narrow")
    normed = norm_rows(whole)
    local_width = attn_width
    head_count = local_width // HEAD_DIM

    projected = add_rows(normed, attn_gathered)
    q_proj = projected[:, :attn_width]
    k_proj = projected[:, attn_width:2 * attn_width]
    v_proj = projected[:, 2 * attn_width:3 * attn_width]
    queries = rotate(q_proj.reshape(tok_rows, head_count, HEAD_DIM), positions).astype(jnp.bfloat16)
    keys_rot = rotate(k_proj.reshape(tok_rows, head_count, HEAD_DIM), positions).astype(
        jnp.bfloat16
    )
    values = v_proj.astype(jnp.bfloat16).reshape(tok_rows, head_count, HEAD_DIM)
    packed = jnp.concatenate([keys_rot, values], axis=2)
    pairs_per_chip = 2
    chips_back = REACH // pairs_per_chip
    line = [shifted(packed, "wide", pairs_per_chip * step) for step in range(1, chips_back + 1)]
    count = lax.axis_size("wide")
    mine = jnp.stack(line + [packed], axis=0)
    partner = lax.ppermute(mine, "wide", [(i, i ^ 1) for i in range(count)])
    partner_rank = wide_rank ^ 1
    block_ids = []
    for rank in (wide_rank, partner_rank):
        block_ids += [rank - pairs_per_chip * step for step in range(1, chips_back + 1)] + [rank]
    kv_all = jnp.concatenate([mine, partner], axis=0).reshape((-1,) + packed.shape[1:])
    key_index = (
        jnp.stack(block_ids)[:, None] * tok_rows + local_index[None, :]
    ).reshape(-1)
    query_index = wide_rank * tok_rows + local_index
    query_start = query_index - positions
    allowed = (key_index[None, :] >= query_start[:, None]) & (key_index[None, :] <= query_index[:, None])
    score_scale = HEAD_DIM ** (-0.5)
    key_all = kv_all[:, :, :HEAD_DIM]
    value_all = kv_all[:, :, HEAD_DIM:]
    scores = (
        jnp.einsum("qhd,khd->hqk", queries, key_all, preferred_element_type=jnp.float32)
        * score_scale
    )
    scores = jnp.where(allowed[None], scores, -1e30)
    row_peak = jnp.max(scores, axis=-1, keepdims=True)
    exps = jnp.where(allowed[None], jnp.exp(scores - row_peak), 0.0)
    attn_probs = (exps / jnp.sum(exps, axis=-1, keepdims=True)).astype(jnp.bfloat16)
    mixed = jnp.einsum("hqk,khd->qhd", attn_probs, value_all, preferred_element_type=jnp.float32)
    attended = mixed.astype(jnp.bfloat16).reshape(tok_rows, local_width)
    attn_terms = lax.dot_general(
        attended, wo_t, (((1,), (1,)), ((), ())), preferred_element_type=jnp.float32
    )
    attn_sum = swap_sum(attn_terms.astype(jnp.bfloat16), "narrow")
    first_res = (hidden_in.astype(jnp.float32) + attn_sum).astype(jnp.bfloat16)
    whole_two = swap_gather(first_res, "narrow")
    normed_two = norm_rows(whole_two)

    gate_proj = add_rows(normed_two, wg_all)
    up_proj = add_rows(normed_two, wu_all)
    hidden = (jax.nn.silu(gate_proj) * up_proj).astype(jnp.bfloat16)
    down_terms = lax.dot_general(
        hidden, wd_t, (((1,), (1,)), ((), ())), preferred_element_type=jnp.float32
    )
    down_sum = swap_sum(down_terms.astype(jnp.bfloat16), "narrow")
    result = (first_res.astype(jnp.float32) + down_sum).astype(jnp.bfloat16)
    page_count = tok_rows // PAGE
    slots = page_table - wide_rank * page_count
    pairs = jnp.stack(
        [
            keys_rot.reshape(page_count, PAGE, local_width),
            values.reshape(page_count, PAGE, local_width),
        ],
        axis=0,
    )
    kv_cache = jnp.zeros_like(pairs).at[:, slots].set(pairs)
    return (result, kv_cache)


def solution(mesh):
    return jax.shard_map(
        per_device,
        mesh=mesh,
        in_specs=(
            P("wide", "narrow"),
            P("wide"),
            P("wide"),
            P("wide", "narrow"),
            P("wide", "narrow"),
            P("wide", "narrow"),
            P("narrow", "wide"),
            P("wide", "narrow"),
            P("wide", "narrow"),
            P("narrow", "wide"),
        ),
        out_specs=(P("wide", "narrow"), P(None, "wide", None, "narrow")),
        check_vma=False,
    )
```

```python
import jax
import jax.numpy as jnp
from jax import lax
from jax.sharding import PartitionSpec as P

HEAD_DIM = 128
REACH = 8
PAGE = 16


epsilon = 1e-05
rope_base = 10000.0


def shifted(value, axis, steps):
    count = lax.axis_size(axis)
    first, last = (max(0, -steps), min(count, count - steps))
    return lax.ppermute(value, axis, [(source, source + steps) for source in range(first, last)])


def swap_gather(value, axis):
    count = lax.axis_size(axis)
    rows, cols = value.shape
    copies = jnp.broadcast_to(value[None], (count, rows, cols))
    got = lax.all_to_all(copies, axis, 0, 0, tiled=True)
    return jnp.moveaxis(got, 0, 1).reshape(rows, cols * count)


def swap_sum(value, axis):
    count = lax.axis_size(axis)
    rows, width = value.shape
    cols = width // count
    pieces = jnp.moveaxis(value.reshape(rows, count, cols), 1, 0)
    got = lax.all_to_all(pieces, axis, 0, 0, tiled=True)
    return jnp.sum(got.astype(jnp.float32), axis=0)


def norm_rows(source):
    widened = source.astype(jnp.float32)
    center = widened - jnp.mean(widened, axis=-1, keepdims=True)
    spread = jnp.mean(center * center, axis=-1, keepdims=True)
    return (center * lax.rsqrt(spread + epsilon)).astype(jnp.bfloat16)


def rotate(projected, positions):
    head_size = projected.shape[-1]
    half_dim = head_size // 2
    frequency = jnp.power(rope_base, -jnp.arange(half_dim, dtype=jnp.float32) * 2.0 / head_size)
    angles = positions.astype(jnp.float32)[:, None] * frequency[None, :]
    cosine = jnp.cos(angles)[:, None, :]
    sine_part = jnp.sin(angles)[:, None, :]
    first_half = projected[..., :half_dim]
    second_half = projected[..., half_dim:]
    return jnp.concatenate(
        [
            first_half * cosine - second_half * sine_part,
            second_half * cosine + first_half * sine_part,
        ],
        axis=-1,
    )


def add_rows(source, piece):
    return jnp.dot(source, piece, preferred_element_type=jnp.float32)


def per_device(hidden_in, segment_ids, page_table, wq, wk, wv, wo, wg, wu, wd):
    tok_rows = hidden_in.shape[0]
    wide_rank = lax.axis_index("wide")
    local_index = jnp.arange(tok_rows, dtype=jnp.int32)

    attn_width = wq.shape[1]

    def gather_pieces(pieces):
        widths = [piece.shape[1] for piece in pieces]
        gathered = lax.all_gather(jnp.concatenate(pieces, axis=1), "wide", axis=0, tiled=True)
        offsets = [sum(widths[:k]) for k in range(len(widths))]
        return [gathered[:, o:o + w] for o, w in zip(offsets, widths)]

    attn_pieces = [wq, wk, wv, wo.T]
    attn_gathered = lax.all_gather(jnp.concatenate(attn_pieces, axis=1), "wide", axis=0, tiled=True)
    wo_t = attn_gathered[:, 3 * attn_width:]
    wg_all, wu_all, wd_t = gather_pieces([wg, wu, wd.T])

    id_blocks = []
    for step_back in range(REACH, 0, -1):
        got = shifted(segment_ids, "wide", step_back)
        id_blocks.append(jnp.where(wide_rank >= step_back, got, -1))
    id_blocks.append(segment_ids)
    window_ids = jnp.concatenate(id_blocks, axis=0)
    window_len = window_ids.shape[0]
    lead = REACH * tok_rows
    window_index = jnp.arange(window_len, dtype=jnp.int32)
    same = window_ids[None, :] == segment_ids[:, None]
    earlier = same & (window_index[None, :] < lead + local_index[:, None])
    positions = jnp.sum(earlier.astype(jnp.int32), axis=1)

    pairs_per_chip = 2
    chips_back = REACH // pairs_per_chip
    partner_rank = wide_rank ^ 1
    block_ids = []
    for step in range(chips_back, 0, -1):
        block_ids += [wide_rank - pairs_per_chip * step, partner_rank - pairs_per_chip * step]
    block_ids += [partner_rank, wide_rank]
    key_index = (
        jnp.stack(block_ids)[:, None] * tok_rows + local_index[None, :]
    ).reshape(-1)
    query_index = wide_rank * tok_rows + local_index
    query_start = query_index - positions
    allowed = (key_index[None, :] >= query_start[:, None]) & (key_index[None, :] <= query_index[:, None])
    allowed, hidden_sent = lax.optimization_barrier((allowed, hidden_in))

    whole = swap_gather(hidden_sent, "narrow")
    normed = norm_rows(whole)
    local_width = attn_width
    head_count = local_width // HEAD_DIM

    projected = add_rows(normed, attn_gathered)
    q_proj = projected[:, :attn_width]
    k_proj = projected[:, attn_width:2 * attn_width]
    v_proj = projected[:, 2 * attn_width:3 * attn_width]
    queries = rotate(q_proj.reshape(tok_rows, head_count, HEAD_DIM), positions).astype(jnp.bfloat16)
    keys_rot = rotate(k_proj.reshape(tok_rows, head_count, HEAD_DIM), positions).astype(
        jnp.bfloat16
    )
    values = v_proj.astype(jnp.bfloat16).reshape(tok_rows, head_count, HEAD_DIM)
    packed = jnp.concatenate([keys_rot, values], axis=2)
    line = [shifted(packed, "wide", pairs_per_chip * step) for step in range(1, chips_back + 1)]
    count = lax.axis_size("wide")
    partner = lax.ppermute(
        jnp.stack(line + [packed], axis=0), "wide", [(i, i ^ 1) for i in range(count)]
    )
    order = []
    for step in range(chips_back, 0, -1):
        order += [line[step - 1], partner[step - 1]]
    order += [partner[chips_back], packed]
    kv_all = jnp.concatenate(order, axis=0)
    score_scale = HEAD_DIM ** (-0.5)
    key_all = kv_all[:, :, :HEAD_DIM]
    value_all = kv_all[:, :, HEAD_DIM:]
    scores = (
        jnp.einsum("qhd,khd->hqk", queries, key_all, preferred_element_type=jnp.float32)
        * score_scale
    )
    scores = jnp.where(allowed[None], scores, -1e30)
    row_peak = jnp.max(scores, axis=-1, keepdims=True)
    exps = jnp.where(allowed[None], jnp.exp(scores - row_peak), 0.0)
    attn_probs = (exps / jnp.sum(exps, axis=-1, keepdims=True)).astype(jnp.bfloat16)
    mixed = jnp.einsum("hqk,khd->qhd", attn_probs, value_all, preferred_element_type=jnp.float32)
    attended = mixed.astype(jnp.bfloat16).reshape(tok_rows, local_width)
    attn_terms = lax.dot_general(
        attended, wo_t, (((1,), (1,)), ((), ())), preferred_element_type=jnp.float32
    )
    attn_sum = swap_sum(attn_terms.astype(jnp.bfloat16), "narrow")
    first_res = (hidden_in.astype(jnp.float32) + attn_sum).astype(jnp.bfloat16)
    whole_two = swap_gather(first_res, "narrow")
    normed_two = norm_rows(whole_two)

    gate_proj = add_rows(normed_two, wg_all)
    up_proj = add_rows(normed_two, wu_all)
    hidden = (jax.nn.silu(gate_proj) * up_proj).astype(jnp.bfloat16)
    down_terms = lax.dot_general(
        hidden, wd_t, (((1,), (1,)), ((), ())), preferred_element_type=jnp.float32
    )
    down_sum = swap_sum(down_terms.astype(jnp.bfloat16), "narrow")
    result = (first_res.astype(jnp.float32) + down_sum).astype(jnp.bfloat16)
    page_count = tok_rows // PAGE
    slots = page_table - wide_rank * page_count
    pairs = jnp.stack(
        [
            keys_rot.reshape(page_count, PAGE, local_width),
            values.reshape(page_count, PAGE, local_width),
        ],
        axis=0,
    )
    kv_cache = jnp.zeros_like(pairs).at[:, slots].set(pairs)
    return (result, kv_cache)


def solution(mesh):
    return jax.shard_map(
        per_device,
        mesh=mesh,
        in_specs=(
            P("wide", "narrow"),
            P("wide"),
            P("wide"),
            P("wide", "narrow"),
            P("wide", "narrow"),
            P("wide", "narrow"),
            P("narrow", "wide"),
            P("wide", "narrow"),
            P("wide", "narrow"),
            P("narrow", "wide"),
        ),
        out_specs=(P("wide", "narrow"), P(None, "wide", None, "narrow")),
        check_vma=False,
    )
```

```python
import jax
import jax.numpy as jnp
from jax import lax
from jax.sharding import PartitionSpec as P

HEAD_DIM = 128
REACH = 8
PAGE = 16


epsilon = 1e-05
rope_base = 10000.0


def shifted(value, axis, steps):
    count = lax.axis_size(axis)
    first, last = (max(0, -steps), min(count, count - steps))
    return lax.ppermute(value, axis, [(source, source + steps) for source in range(first, last)])


def swap_gather(value, axis):
    count = lax.axis_size(axis)
    rows, cols = value.shape
    copies = jnp.broadcast_to(value[None], (count, rows, cols))
    got = lax.all_to_all(copies, axis, 0, 0, tiled=True)
    return jnp.moveaxis(got, 0, 1).reshape(rows, cols * count)


def swap_sum(value, axis):
    count = lax.axis_size(axis)
    rows, width = value.shape
    cols = width // count
    pieces = jnp.moveaxis(value.reshape(rows, count, cols), 1, 0)
    got = lax.all_to_all(pieces, axis, 0, 0, tiled=True)
    return jnp.sum(got.astype(jnp.float32), axis=0)


def norm_rows(source):
    widened = source.astype(jnp.float32)
    center = widened - jnp.mean(widened, axis=-1, keepdims=True)
    spread = jnp.mean(center * center, axis=-1, keepdims=True)
    return (center * lax.rsqrt(spread + epsilon)).astype(jnp.bfloat16)


def rotate(projected, positions):
    head_size = projected.shape[-1]
    half_dim = head_size // 2
    frequency = jnp.power(rope_base, -jnp.arange(half_dim, dtype=jnp.float32) * 2.0 / head_size)
    angles = positions.astype(jnp.float32)[:, None] * frequency[None, :]
    cosine = jnp.cos(angles)[:, None, :]
    sine_part = jnp.sin(angles)[:, None, :]
    first_half = projected[..., :half_dim]
    second_half = projected[..., half_dim:]
    return jnp.concatenate(
        [
            first_half * cosine - second_half * sine_part,
            second_half * cosine + first_half * sine_part,
        ],
        axis=-1,
    )


def add_rows(source, piece):
    return jnp.dot(source, piece, preferred_element_type=jnp.float32)


def per_device(hidden_in, segment_ids, page_table, wq, wk, wv, wo, wg, wu, wd):
    tok_rows = hidden_in.shape[0]
    wide_rank = lax.axis_index("wide")
    local_index = jnp.arange(tok_rows, dtype=jnp.int32)

    attn_width = wq.shape[1]

    def gather_pieces(pieces):
        widths = [piece.shape[1] for piece in pieces]
        gathered = lax.all_gather(jnp.concatenate(pieces, axis=1), "wide", axis=0, tiled=True)
        offsets = [sum(widths[:k]) for k in range(len(widths))]
        return [gathered[:, o:o + w] for o, w in zip(offsets, widths)]

    attn_pieces = [wq, wk, wv, wo.T]
    attn_gathered = lax.all_gather(jnp.concatenate(attn_pieces, axis=1), "wide", axis=0, tiled=True)
    wo_t = attn_gathered[:, 3 * attn_width:]
    wg_all, wu_all, wd_t = gather_pieces([wg, wu, wd.T])

    id_blocks = []
    for step_back in range(REACH, 0, -1):
        got = shifted(segment_ids, "wide", step_back)
        id_blocks.append(jnp.where(wide_rank >= step_back, got, -1))
    id_blocks.append(segment_ids)
    window_ids = jnp.concatenate(id_blocks, axis=0)
    window_len = window_ids.shape[0]
    lead = REACH * tok_rows
    window_index = jnp.arange(window_len, dtype=jnp.int32)
    same = window_ids[None, :] == segment_ids[:, None]
    earlier = same & (window_index[None, :] < lead + local_index[:, None])
    positions = jnp.sum(earlier.astype(jnp.int32), axis=1)

    pairs_per_chip = 2
    chips_back = REACH // pairs_per_chip
    partner_rank = wide_rank ^ 1
    block_ids = []
    for step in range(chips_back, 0, -1):
        block_ids += [wide_rank - pairs_per_chip * step, partner_rank - pairs_per_chip * step]
    block_ids += [partner_rank, wide_rank]
    key_index = (
        jnp.stack(block_ids)[:, None] * tok_rows + local_index[None, :]
    ).reshape(-1)
    query_index = wide_rank * tok_rows + local_index
    query_start = query_index - positions
    allowed = (key_index[None, :] >= query_start[:, None]) & (key_index[None, :] <= query_index[:, None])
    allowed, hidden_sent = lax.optimization_barrier((allowed, hidden_in))

    whole = swap_gather(hidden_sent, "narrow")
    normed = norm_rows(whole)
    local_width = attn_width
    head_count = local_width // HEAD_DIM

    projected = add_rows(normed, attn_gathered)
    q_proj = projected[:, :attn_width]
    k_proj = projected[:, attn_width:2 * attn_width]
    v_proj = projected[:, 2 * attn_width:3 * attn_width]
    queries = rotate(q_proj.reshape(tok_rows, head_count, HEAD_DIM), positions).astype(jnp.bfloat16)
    keys_rot = rotate(k_proj.reshape(tok_rows, head_count, HEAD_DIM), positions).astype(
        jnp.bfloat16
    )
    values = v_proj.astype(jnp.bfloat16).reshape(tok_rows, head_count, HEAD_DIM)
    packed = jnp.transpose(jnp.concatenate([keys_rot, values], axis=2), (1, 2, 0))
    line = [shifted(packed, "wide", pairs_per_chip * step) for step in range(1, chips_back + 1)]
    count = lax.axis_size("wide")
    partner = lax.ppermute(
        jnp.stack(line + [packed], axis=0), "wide", [(i, i ^ 1) for i in range(count)]
    )
    order = []
    for step in range(chips_back, 0, -1):
        order += [line[step - 1], partner[step - 1]]
    order += [partner[chips_back], packed]
    kv_all = jnp.concatenate(order, axis=-1)
    score_scale = HEAD_DIM ** (-0.5)
    key_all = kv_all[:, :HEAD_DIM, :]
    value_all = kv_all[:, HEAD_DIM:, :]
    scores = (
        jnp.einsum("qhd,hdk->hqk", queries, key_all, preferred_element_type=jnp.float32)
        * score_scale
    )
    scores = jnp.where(allowed[None], scores, -1e30)
    row_peak = jnp.max(scores, axis=-1, keepdims=True)
    exps = jnp.where(allowed[None], jnp.exp(scores - row_peak), 0.0)
    attn_probs = (exps / jnp.sum(exps, axis=-1, keepdims=True)).astype(jnp.bfloat16)
    mixed = jnp.einsum("hqk,hdk->qhd", attn_probs, value_all, preferred_element_type=jnp.float32)
    attended = mixed.astype(jnp.bfloat16).reshape(tok_rows, local_width)
    attn_terms = lax.dot_general(
        attended, wo_t, (((1,), (1,)), ((), ())), preferred_element_type=jnp.float32
    )
    attn_sum = swap_sum(attn_terms.astype(jnp.bfloat16), "narrow")
    first_res = (hidden_in.astype(jnp.float32) + attn_sum).astype(jnp.bfloat16)
    whole_two = swap_gather(first_res, "narrow")
    normed_two = norm_rows(whole_two)

    gate_proj = add_rows(normed_two, wg_all)
    up_proj = add_rows(normed_two, wu_all)
    hidden = (jax.nn.silu(gate_proj) * up_proj).astype(jnp.bfloat16)
    down_terms = lax.dot_general(
        hidden, wd_t, (((1,), (1,)), ((), ())), preferred_element_type=jnp.float32
    )
    down_sum = swap_sum(down_terms.astype(jnp.bfloat16), "narrow")
    result = (first_res.astype(jnp.float32) + down_sum).astype(jnp.bfloat16)
    page_count = tok_rows // PAGE
    slots = page_table - wide_rank * page_count
    pairs = jnp.stack(
        [
            keys_rot.reshape(page_count, PAGE, local_width),
            values.reshape(page_count, PAGE, local_width),
        ],
        axis=0,
    )
    kv_cache = jnp.zeros_like(pairs).at[:, slots].set(pairs)
    return (result, kv_cache)


def solution(mesh):
    return jax.shard_map(
        per_device,
        mesh=mesh,
        in_specs=(
            P("wide", "narrow"),
            P("wide"),
            P("wide"),
            P("wide", "narrow"),
            P("wide", "narrow"),
            P("wide", "narrow"),
            P("narrow", "wide"),
            P("wide", "narrow"),
            P("wide", "narrow"),
            P("narrow", "wide"),
        ),
        out_specs=(P("wide", "narrow"), P(None, "wide", None, "narrow")),
        check_vma=False,
    )
```

```python
import jax
import jax.numpy as jnp
from jax import lax
from jax.sharding import PartitionSpec as P

HEAD_DIM = 128
REACH = 8
PAGE = 16


epsilon = 1e-05
rope_base = 10000.0


def shifted(value, axis, steps):
    count = lax.axis_size(axis)
    first, last = (max(0, -steps), min(count, count - steps))
    return lax.ppermute(value, axis, [(source, source + steps) for source in range(first, last)])


def swap_gather(value, axis):
    count = lax.axis_size(axis)
    rows, cols = value.shape
    copies = jnp.broadcast_to(value[None], (count, rows, cols))
    got = lax.all_to_all(copies, axis, 0, 0, tiled=True)
    return jnp.moveaxis(got, 0, 1).reshape(rows, cols * count)


def swap_sum(value, axis):
    count = lax.axis_size(axis)
    rows, width = value.shape
    cols = width // count
    pieces = jnp.moveaxis(value.reshape(rows, count, cols), 1, 0)
    got = lax.all_to_all(pieces, axis, 0, 0, tiled=True)
    return jnp.sum(got.astype(jnp.float32), axis=0)


def norm_rows(source):
    widened = source.astype(jnp.float32)
    center = widened - jnp.mean(widened, axis=-1, keepdims=True)
    spread = jnp.mean(center * center, axis=-1, keepdims=True)
    return (center * lax.rsqrt(spread + epsilon)).astype(jnp.bfloat16)


def rotate(projected, positions):
    head_size = projected.shape[-1]
    half_dim = head_size // 2
    frequency = jnp.power(rope_base, -jnp.arange(half_dim, dtype=jnp.float32) * 2.0 / head_size)
    angles = positions.astype(jnp.float32)[:, None] * frequency[None, :]
    cosine = jnp.cos(angles)[:, None, :]
    sine_part = jnp.sin(angles)[:, None, :]
    first_half = projected[..., :half_dim]
    second_half = projected[..., half_dim:]
    return jnp.concatenate(
        [
            first_half * cosine - second_half * sine_part,
            second_half * cosine + first_half * sine_part,
        ],
        axis=-1,
    )


def add_rows(source, piece):
    return jnp.dot(source, piece, preferred_element_type=jnp.float32)


def per_device(hidden_in, segment_ids, page_table, wq, wk, wv, wo, wg, wu, wd):
    tok_rows = hidden_in.shape[0]
    wide_rank = lax.axis_index("wide")
    local_index = jnp.arange(tok_rows, dtype=jnp.int32)

    attn_width = wq.shape[1]

    def gather_pieces(pieces):
        widths = [piece.shape[1] for piece in pieces]
        gathered = lax.all_gather(jnp.concatenate(pieces, axis=1), "wide", axis=0, tiled=True)
        offsets = [sum(widths[:k]) for k in range(len(widths))]
        return [gathered[:, o:o + w] for o, w in zip(offsets, widths)]

    attn_pieces = [wq, wk, wv, wo.T]
    attn_gathered = lax.all_gather(jnp.concatenate(attn_pieces, axis=1), "wide", axis=0, tiled=True)
    wo_t = attn_gathered[:, 3 * attn_width:]
    wg_all, wu_all, wd_t = gather_pieces([wg, wu, wd.T])

    id_blocks = []
    for step_back in range(REACH, 0, -1):
        got = shifted(segment_ids, "wide", step_back)
        id_blocks.append(jnp.where(wide_rank >= step_back, got, -1))
    id_blocks.append(segment_ids)
    window_ids = jnp.concatenate(id_blocks, axis=0)
    window_len = window_ids.shape[0]
    lead = REACH * tok_rows
    window_index = jnp.arange(window_len, dtype=jnp.int32)
    same = window_ids[None, :] == segment_ids[:, None]
    earlier = same & (window_index[None, :] < lead + local_index[:, None])
    positions = jnp.sum(earlier.astype(jnp.int32), axis=1)

    pairs_per_chip = 2
    chips_back = REACH // pairs_per_chip
    partner_rank = wide_rank ^ 1
    first_core = (wide_rank % pairs_per_chip) == 0
    block_ids = [
        wide_rank - pairs_per_chip * chips_back,
        jnp.where(first_core, partner_rank - pairs_per_chip * chips_back, partner_rank),
    ]
    for step in range(chips_back - 1, 0, -1):
        block_ids += [wide_rank - pairs_per_chip * step, partner_rank - pairs_per_chip * step]
    block_ids += [wide_rank]
    key_index = (
        jnp.stack(block_ids)[:, None] * tok_rows + local_index[None, :]
    ).reshape(-1)
    query_index = wide_rank * tok_rows + local_index
    query_start = query_index - positions
    allowed = (key_index[None, :] >= query_start[:, None]) & (key_index[None, :] <= query_index[:, None])
    allowed, hidden_sent = lax.optimization_barrier((allowed, hidden_in))

    whole = swap_gather(hidden_sent, "narrow")
    normed = norm_rows(whole)
    local_width = attn_width
    head_count = local_width // HEAD_DIM

    projected = add_rows(normed, attn_gathered)
    q_proj = projected[:, :attn_width]
    k_proj = projected[:, attn_width:2 * attn_width]
    v_proj = projected[:, 2 * attn_width:3 * attn_width]
    queries = rotate(q_proj.reshape(tok_rows, head_count, HEAD_DIM), positions).astype(jnp.bfloat16)
    keys_rot = rotate(k_proj.reshape(tok_rows, head_count, HEAD_DIM), positions).astype(
        jnp.bfloat16
    )
    values = v_proj.astype(jnp.bfloat16).reshape(tok_rows, head_count, HEAD_DIM)
    packed = jnp.transpose(jnp.concatenate([keys_rot, values], axis=2), (1, 2, 0))
    line = [shifted(packed, "wide", pairs_per_chip * step) for step in range(1, chips_back + 1)]
    count = lax.axis_size("wide")
    partner = lax.ppermute(
        jnp.stack(line + [packed], axis=0), "wide", [(i, i ^ 1) for i in range(count)]
    )
    order = [line[chips_back - 1], jnp.where(first_core, partner[chips_back - 1], partner[chips_back])]
    for step in range(chips_back - 1, 0, -1):
        order += [line[step - 1], partner[step - 1]]
    order += [packed]
    kv_all = jnp.concatenate(order, axis=-1)
    score_scale = HEAD_DIM ** (-0.5)
    key_all = kv_all[:, :HEAD_DIM, :]
    value_all = kv_all[:, HEAD_DIM:, :]
    scores = (
        jnp.einsum("qhd,hdk->hqk", queries, key_all, preferred_element_type=jnp.float32)
        * score_scale
    )
    scores = jnp.where(allowed[None], scores, -1e30)
    row_peak = jnp.max(scores, axis=-1, keepdims=True)
    exps = jnp.where(allowed[None], jnp.exp(scores - row_peak), 0.0)
    attn_probs = (exps / jnp.sum(exps, axis=-1, keepdims=True)).astype(jnp.bfloat16)
    mixed = jnp.einsum("hqk,hdk->qhd", attn_probs, value_all, preferred_element_type=jnp.float32)
    attended = mixed.astype(jnp.bfloat16).reshape(tok_rows, local_width)
    attn_terms = lax.dot_general(
        attended, wo_t, (((1,), (1,)), ((), ())), preferred_element_type=jnp.float32
    )
    attn_sum = swap_sum(attn_terms.astype(jnp.bfloat16), "narrow")
    first_res = (hidden_in.astype(jnp.float32) + attn_sum).astype(jnp.bfloat16)
    whole_two = swap_gather(first_res, "narrow")
    normed_two = norm_rows(whole_two)

    gate_proj = add_rows(normed_two, wg_all)
    up_proj = add_rows(normed_two, wu_all)
    hidden = (jax.nn.silu(gate_proj) * up_proj).astype(jnp.bfloat16)
    down_terms = lax.dot_general(
        hidden, wd_t, (((1,), (1,)), ((), ())), preferred_element_type=jnp.float32
    )
    down_sum = swap_sum(down_terms.astype(jnp.bfloat16), "narrow")
    result = (first_res.astype(jnp.float32) + down_sum).astype(jnp.bfloat16)
    page_count = tok_rows // PAGE
    slots = page_table - wide_rank * page_count
    pairs = jnp.stack(
        [
            keys_rot.reshape(page_count, PAGE, local_width),
            values.reshape(page_count, PAGE, local_width),
        ],
        axis=0,
    )
    kv_cache = jnp.zeros_like(pairs).at[:, slots].set(pairs)
    return (result, kv_cache)


def solution(mesh):
    return jax.shard_map(
        per_device,
        mesh=mesh,
        in_specs=(
            P("wide", "narrow"),
            P("wide"),
            P("wide"),
            P("wide", "narrow"),
            P("wide", "narrow"),
            P("wide", "narrow"),
            P("narrow", "wide"),
            P("wide", "narrow"),
            P("wide", "narrow"),
            P("narrow", "wide"),
        ),
        out_specs=(P("wide", "narrow"), P(None, "wide", None, "narrow")),
        check_vma=False,
    )
```

```python
import jax
import jax.numpy as jnp
from jax import lax
from jax.sharding import PartitionSpec as P

HEAD_DIM = 128
REACH = 8
PAGE = 16


epsilon = 1e-05
rope_base = 10000.0


def shifted(value, axis, steps):
    count = lax.axis_size(axis)
    first, last = (max(0, -steps), min(count, count - steps))
    return lax.ppermute(value, axis, [(source, source + steps) for source in range(first, last)])


def swap_gather(value, axis):
    count = lax.axis_size(axis)
    rows, cols = value.shape
    copies = jnp.broadcast_to(value[None], (count, rows, cols))
    got = lax.all_to_all(copies, axis, 0, 0, tiled=True)
    return jnp.moveaxis(got, 0, 1).reshape(rows, cols * count)


def swap_sum(value, axis):
    count = lax.axis_size(axis)
    rows, width = value.shape
    cols = width // count
    pieces = jnp.moveaxis(value.reshape(rows, count, cols), 1, 0)
    got = lax.all_to_all(pieces, axis, 0, 0, tiled=True)
    return jnp.sum(got.astype(jnp.float32), axis=0)


def norm_rows(source):
    widened = source.astype(jnp.float32)
    center = widened - jnp.mean(widened, axis=-1, keepdims=True)
    spread = jnp.mean(center * center, axis=-1, keepdims=True)
    return (center * lax.rsqrt(spread + epsilon)).astype(jnp.bfloat16)


def rotate(projected, positions):
    head_size = projected.shape[-1]
    half_dim = head_size // 2
    frequency = jnp.power(rope_base, -jnp.arange(half_dim, dtype=jnp.float32) * 2.0 / head_size)
    angles = positions.astype(jnp.float32)[:, None] * frequency[None, :]
    cosine = jnp.cos(angles)[:, None, :]
    sine_part = jnp.sin(angles)[:, None, :]
    first_half = projected[..., :half_dim]
    second_half = projected[..., half_dim:]
    return jnp.concatenate(
        [
            first_half * cosine - second_half * sine_part,
            second_half * cosine + first_half * sine_part,
        ],
        axis=-1,
    )


def add_rows(source, piece):
    return jnp.dot(source, piece, preferred_element_type=jnp.float32)


def per_device(hidden_in, segment_ids, page_table, wq, wk, wv, wo, wg, wu, wd):
    tok_rows = hidden_in.shape[0]
    wide_rank = lax.axis_index("wide")
    local_index = jnp.arange(tok_rows, dtype=jnp.int32)

    attn_width = wq.shape[1]

    def gather_pieces(pieces):
        widths = [piece.shape[1] for piece in pieces]
        gathered = lax.all_gather(jnp.concatenate(pieces, axis=1), "wide", axis=0, tiled=True)
        offsets = [sum(widths[:k]) for k in range(len(widths))]
        return [gathered[:, o:o + w] for o, w in zip(offsets, widths)]

    attn_pieces = [wq, wk, wv, wo.T]
    attn_gathered = lax.all_gather(jnp.concatenate(attn_pieces, axis=1), "wide", axis=0, tiled=True)
    wo_t = attn_gathered[:, 3 * attn_width:]
    wg_all, wu_all, wd_t = gather_pieces([wg, wu, wd.T])

    id_blocks = []
    for step_back in range(REACH, 0, -1):
        got = shifted(segment_ids, "wide", step_back)
        id_blocks.append(jnp.where(wide_rank >= step_back, got, -1))
    id_blocks.append(segment_ids)
    window_ids = jnp.concatenate(id_blocks, axis=0)
    window_len = window_ids.shape[0]
    lead = REACH * tok_rows
    window_index = jnp.arange(window_len, dtype=jnp.int32)
    same = window_ids[None, :] == segment_ids[:, None]
    earlier = same & (window_index[None, :] < lead + local_index[:, None])
    positions = jnp.sum(earlier.astype(jnp.int32), axis=1)

    pairs_per_chip = 2
    chips_back = REACH // pairs_per_chip
    partner_rank = wide_rank ^ 1
    first_core = (wide_rank % pairs_per_chip) == 0
    block_ids = [
        wide_rank - pairs_per_chip * chips_back,
        jnp.where(first_core, partner_rank - pairs_per_chip * chips_back, partner_rank),
    ]
    for step in range(chips_back - 1, 0, -1):
        block_ids += [wide_rank - pairs_per_chip * step, partner_rank - pairs_per_chip * step]
    block_ids += [wide_rank]
    key_index = (
        jnp.stack(block_ids)[:, None] * tok_rows + local_index[None, :]
    ).reshape(-1)
    query_index = wide_rank * tok_rows + local_index
    query_start = query_index - positions
    allowed = (key_index[None, :] >= query_start[:, None]) & (key_index[None, :] <= query_index[:, None])
    allowed, hidden_sent = lax.optimization_barrier((allowed, hidden_in))

    whole = swap_gather(hidden_sent, "narrow")
    normed = norm_rows(whole)
    local_width = attn_width
    head_count = local_width // HEAD_DIM

    projected = add_rows(normed, attn_gathered)
    q_proj = projected[:, :attn_width]
    k_proj = projected[:, attn_width:2 * attn_width]
    v_proj = projected[:, 2 * attn_width:3 * attn_width]
    queries = rotate(q_proj.reshape(tok_rows, head_count, HEAD_DIM), positions).astype(jnp.bfloat16)
    keys_rot = rotate(k_proj.reshape(tok_rows, head_count, HEAD_DIM), positions).astype(
        jnp.bfloat16
    )
    values = v_proj.astype(jnp.bfloat16).reshape(tok_rows, head_count, HEAD_DIM)
    packed = jnp.transpose(jnp.concatenate([keys_rot, values], axis=2), (1, 2, 0))
    line = [shifted(packed, "wide", pairs_per_chip * step) for step in range(1, chips_back + 1)]
    count = lax.axis_size("wide")
    sent = line[:chips_back - 1] + [jnp.where(first_core, packed, line[chips_back - 1])]
    partner = lax.ppermute(jnp.stack(sent, axis=0), "wide", [(i, i ^ 1) for i in range(count)])
    order = [line[chips_back - 1], partner[chips_back - 1]]
    for step in range(chips_back - 1, 0, -1):
        order += [line[step - 1], partner[step - 1]]
    order += [packed]
    kv_all = jnp.concatenate(order, axis=-1)
    score_scale = HEAD_DIM ** (-0.5)
    key_all = kv_all[:, :HEAD_DIM, :]
    value_all = kv_all[:, HEAD_DIM:, :]
    scores = (
        jnp.einsum("qhd,hdk->hqk", queries, key_all, preferred_element_type=jnp.float32)
        * score_scale
    )
    scores = jnp.where(allowed[None], scores, -1e30)
    row_peak = jnp.max(scores, axis=-1, keepdims=True)
    exps = jnp.where(allowed[None], jnp.exp(scores - row_peak), 0.0)
    attn_probs = (exps / jnp.sum(exps, axis=-1, keepdims=True)).astype(jnp.bfloat16)
    mixed = jnp.einsum("hqk,hdk->qhd", attn_probs, value_all, preferred_element_type=jnp.float32)
    attended = mixed.astype(jnp.bfloat16).reshape(tok_rows, local_width)
    attn_terms = lax.dot_general(
        attended, wo_t, (((1,), (1,)), ((), ())), preferred_element_type=jnp.float32
    )
    attn_sum = swap_sum(attn_terms.astype(jnp.bfloat16), "narrow")
    first_res = (hidden_in.astype(jnp.float32) + attn_sum).astype(jnp.bfloat16)
    whole_two = swap_gather(first_res, "narrow")
    normed_two = norm_rows(whole_two)

    gate_proj = add_rows(normed_two, wg_all)
    up_proj = add_rows(normed_two, wu_all)
    hidden = (jax.nn.silu(gate_proj) * up_proj).astype(jnp.bfloat16)
    down_terms = lax.dot_general(
        hidden, wd_t, (((1,), (1,)), ((), ())), preferred_element_type=jnp.float32
    )
    down_sum = swap_sum(down_terms.astype(jnp.bfloat16), "narrow")
    result = (first_res.astype(jnp.float32) + down_sum).astype(jnp.bfloat16)
    page_count = tok_rows // PAGE
    slots = page_table - wide_rank * page_count
    pairs = jnp.stack(
        [
            keys_rot.reshape(page_count, PAGE, local_width),
            values.reshape(page_count, PAGE, local_width),
        ],
        axis=0,
    )
    kv_cache = jnp.zeros_like(pairs).at[:, slots].set(pairs)
    return (result, kv_cache)


def solution(mesh):
    return jax.shard_map(
        per_device,
        mesh=mesh,
        in_specs=(
            P("wide", "narrow"),
            P("wide"),
            P("wide"),
            P("wide", "narrow"),
            P("wide", "narrow"),
            P("wide", "narrow"),
            P("narrow", "wide"),
            P("wide", "narrow"),
            P("wide", "narrow"),
            P("narrow", "wide"),
        ),
        out_specs=(P("wide", "narrow"), P(None, "wide", None, "narrow")),
        check_vma=False,
    )
```

```python
import jax
import jax.numpy as jnp
from jax import lax
from jax.sharding import PartitionSpec as P

HEAD_DIM = 128
REACH = 8
PAGE = 16


epsilon = 1e-05
rope_base = 10000.0


def shifted(value, axis, steps):
    count = lax.axis_size(axis)
    first, last = (max(0, -steps), min(count, count - steps))
    return lax.ppermute(value, axis, [(source, source + steps) for source in range(first, last)])


def swap_gather(value, axis):
    count = lax.axis_size(axis)
    rows, cols = value.shape
    copies = jnp.broadcast_to(value[None], (count, rows, cols))
    got = lax.all_to_all(copies, axis, 0, 0, tiled=True)
    return jnp.moveaxis(got, 0, 1).reshape(rows, cols * count)


def swap_sum(pieces, axis):
    got = lax.all_to_all(pieces, axis, 0, 0, tiled=True)
    return jnp.sum(got.astype(jnp.float32), axis=0)


def norm_rows(source):
    widened = source.astype(jnp.float32)
    center = widened - jnp.mean(widened, axis=-1, keepdims=True)
    spread = jnp.mean(center * center, axis=-1, keepdims=True)
    return (center * lax.rsqrt(spread + epsilon)).astype(jnp.bfloat16)


def rotate(projected, positions):
    head_size = projected.shape[-1]
    half_dim = head_size // 2
    frequency = jnp.power(rope_base, -jnp.arange(half_dim, dtype=jnp.float32) * 2.0 / head_size)
    angles = positions.astype(jnp.float32)[:, None] * frequency[None, :]
    cosine = jnp.cos(angles)[:, None, :]
    sine_part = jnp.sin(angles)[:, None, :]
    first_half = projected[..., :half_dim]
    second_half = projected[..., half_dim:]
    return jnp.concatenate(
        [
            first_half * cosine - second_half * sine_part,
            second_half * cosine + first_half * sine_part,
        ],
        axis=-1,
    )


def add_rows(source, piece):
    return jnp.dot(source, piece, preferred_element_type=jnp.float32)


def per_device(hidden_in, segment_ids, page_table, wq, wk, wv, wo, wg, wu, wd):
    tok_rows = hidden_in.shape[0]
    wide_rank = lax.axis_index("wide")
    local_index = jnp.arange(tok_rows, dtype=jnp.int32)

    attn_width = wq.shape[1]

    def gather_pieces(pieces):
        widths = [piece.shape[1] for piece in pieces]
        gathered = lax.all_gather(jnp.concatenate(pieces, axis=1), "wide", axis=0, tiled=True)
        offsets = [sum(widths[:k]) for k in range(len(widths))]
        return [gathered[:, o:o + w] for o, w in zip(offsets, widths)]

    attn_pieces = [wq, wk, wv, wo.T]
    attn_gathered = lax.all_gather(jnp.concatenate(attn_pieces, axis=1), "wide", axis=0, tiled=True)
    wo_t = attn_gathered[:, 3 * attn_width:]
    wg_all, wu_all, wd_t = gather_pieces([wg, wu, wd.T])

    id_blocks = []
    for step_back in range(REACH, 0, -1):
        got = shifted(segment_ids, "wide", step_back)
        id_blocks.append(jnp.where(wide_rank >= step_back, got, -1))
    id_blocks.append(segment_ids)
    window_ids = jnp.concatenate(id_blocks, axis=0)
    window_len = window_ids.shape[0]
    lead = REACH * tok_rows
    window_index = jnp.arange(window_len, dtype=jnp.int32)
    same = window_ids[None, :] == segment_ids[:, None]
    earlier = same & (window_index[None, :] < lead + local_index[:, None])
    positions = jnp.sum(earlier.astype(jnp.int32), axis=1)

    pairs_per_chip = 2
    chips_back = REACH // pairs_per_chip
    partner_rank = wide_rank ^ 1
    first_core = (wide_rank % pairs_per_chip) == 0
    block_ids = [
        wide_rank - pairs_per_chip * chips_back,
        jnp.where(first_core, partner_rank - pairs_per_chip * chips_back, partner_rank),
    ]
    for step in range(chips_back - 1, 0, -1):
        block_ids += [wide_rank - pairs_per_chip * step, partner_rank - pairs_per_chip * step]
    block_ids += [wide_rank]
    key_index = (
        jnp.stack(block_ids)[:, None] * tok_rows + local_index[None, :]
    ).reshape(-1)
    query_index = wide_rank * tok_rows + local_index
    query_start = query_index - positions
    allowed = (key_index[None, :] >= query_start[:, None]) & (key_index[None, :] <= query_index[:, None])
    allowed, hidden_sent = lax.optimization_barrier((allowed, hidden_in))

    whole = swap_gather(hidden_sent, "narrow")
    normed = norm_rows(whole)
    local_width = attn_width
    head_count = local_width // HEAD_DIM

    projected = add_rows(normed, attn_gathered)
    q_proj = projected[:, :attn_width]
    k_proj = projected[:, attn_width:2 * attn_width]
    v_proj = projected[:, 2 * attn_width:3 * attn_width]
    queries = rotate(q_proj.reshape(tok_rows, head_count, HEAD_DIM), positions).astype(jnp.bfloat16)
    keys_rot = rotate(k_proj.reshape(tok_rows, head_count, HEAD_DIM), positions).astype(
        jnp.bfloat16
    )
    values = v_proj.astype(jnp.bfloat16).reshape(tok_rows, head_count, HEAD_DIM)
    packed = jnp.transpose(jnp.concatenate([keys_rot, values], axis=2), (1, 2, 0))
    line = [shifted(packed, "wide", pairs_per_chip * step) for step in range(1, chips_back + 1)]
    count = lax.axis_size("wide")
    partner = lax.ppermute(
        jnp.stack(line + [packed], axis=0), "wide", [(i, i ^ 1) for i in range(count)]
    )
    order = [line[chips_back - 1], jnp.where(first_core, partner[chips_back - 1], partner[chips_back])]
    for step in range(chips_back - 1, 0, -1):
        order += [line[step - 1], partner[step - 1]]
    order += [packed]
    kv_all = jnp.concatenate(order, axis=-1)
    score_scale = HEAD_DIM ** (-0.5)
    key_all = kv_all[:, :HEAD_DIM, :]
    value_all = kv_all[:, HEAD_DIM:, :]
    scores = (
        jnp.einsum("qhd,hdk->hqk", queries, key_all, preferred_element_type=jnp.float32)
        * score_scale
    )
    scores = jnp.where(allowed[None], scores, -1e30)
    row_peak = jnp.max(scores, axis=-1, keepdims=True)
    exps = jnp.where(allowed[None], jnp.exp(scores - row_peak), 0.0)
    attn_probs = (exps / jnp.sum(exps, axis=-1, keepdims=True)).astype(jnp.bfloat16)
    mixed = jnp.einsum("hqk,hdk->qhd", attn_probs, value_all, preferred_element_type=jnp.float32)
    attended = mixed.astype(jnp.bfloat16).reshape(tok_rows, local_width)
    narrow_count = lax.axis_size("narrow")
    attn_terms = jnp.einsum(
        "tc,goc->gto", attended, wo_t.reshape(narrow_count, -1, wo_t.shape[1]),
        preferred_element_type=jnp.float32,
    )
    attn_sum = swap_sum(attn_terms.astype(jnp.bfloat16), "narrow")
    first_res = (hidden_in.astype(jnp.float32) + attn_sum).astype(jnp.bfloat16)
    whole_two = swap_gather(first_res, "narrow")
    normed_two = norm_rows(whole_two)

    gate_proj = add_rows(normed_two, wg_all)
    up_proj = add_rows(normed_two, wu_all)
    hidden = (jax.nn.silu(gate_proj) * up_proj).astype(jnp.bfloat16)
    down_terms = jnp.einsum(
        "tc,goc->gto", hidden, wd_t.reshape(narrow_count, -1, wd_t.shape[1]),
        preferred_element_type=jnp.float32,
    )
    down_sum = swap_sum(down_terms.astype(jnp.bfloat16), "narrow")
    result = (first_res.astype(jnp.float32) + down_sum).astype(jnp.bfloat16)
    page_count = tok_rows // PAGE
    slots = page_table - wide_rank * page_count
    pairs = jnp.stack(
        [
            keys_rot.reshape(page_count, PAGE, local_width),
            values.reshape(page_count, PAGE, local_width),
        ],
        axis=0,
    )
    kv_cache = jnp.zeros_like(pairs).at[:, slots].set(pairs)
    return (result, kv_cache)


def solution(mesh):
    return jax.shard_map(
        per_device,
        mesh=mesh,
        in_specs=(
            P("wide", "narrow"),
            P("wide"),
            P("wide"),
            P("wide", "narrow"),
            P("wide", "narrow"),
            P("wide", "narrow"),
            P("narrow", "wide"),
            P("wide", "narrow"),
            P("wide", "narrow"),
            P("narrow", "wide"),
        ),
        out_specs=(P("wide", "narrow"), P(None, "wide", None, "narrow")),
        check_vma=False,
    )
```

```python
import jax
import jax.numpy as jnp
from jax import lax
from jax.sharding import PartitionSpec as P

HEAD_DIM = 128
REACH = 8
PAGE = 16


epsilon = 1e-05
rope_base = 10000.0


def shifted(value, axis, steps):
    count = lax.axis_size(axis)
    first, last = (max(0, -steps), min(count, count - steps))
    return lax.ppermute(value, axis, [(source, source + steps) for source in range(first, last)])


def swap_gather(value, axis):
    count = lax.axis_size(axis)
    rows, cols = value.shape
    copies = jnp.broadcast_to(value[None], (count, rows, cols))
    got = lax.all_to_all(copies, axis, 0, 0, tiled=True)
    return jnp.moveaxis(got, 0, 1).reshape(rows, cols * count)


def swap_sum(pieces, axis):
    got = lax.all_to_all(pieces, axis, 0, 0, tiled=True)
    return jnp.sum(got.astype(jnp.float32), axis=0)


def norm_rows(source):
    widened = source.astype(jnp.float32)
    center = widened - jnp.mean(widened, axis=-1, keepdims=True)
    spread = jnp.mean(center * center, axis=-1, keepdims=True)
    return (center * lax.rsqrt(spread + epsilon)).astype(jnp.bfloat16)


def rotate(projected, positions):
    head_size = projected.shape[-1]
    half_dim = head_size // 2
    frequency = jnp.power(rope_base, -jnp.arange(half_dim, dtype=jnp.float32) * 2.0 / head_size)
    angles = positions.astype(jnp.float32)[:, None] * frequency[None, :]
    cosine = jnp.cos(angles)[:, None, :]
    sine_part = jnp.sin(angles)[:, None, :]
    first_half = projected[..., :half_dim]
    second_half = projected[..., half_dim:]
    return jnp.concatenate(
        [
            first_half * cosine - second_half * sine_part,
            second_half * cosine + first_half * sine_part,
        ],
        axis=-1,
    )


def add_rows(source, piece):
    return jnp.dot(source, piece, preferred_element_type=jnp.float32)


def per_device(hidden_in, segment_ids, page_table, wq, wk, wv, wo, wg, wu, wd):
    tok_rows = hidden_in.shape[0]
    wide_rank = lax.axis_index("wide")
    local_index = jnp.arange(tok_rows, dtype=jnp.int32)

    attn_width = wq.shape[1]

    def gather_pieces(pieces):
        widths = [piece.shape[1] for piece in pieces]
        gathered = lax.all_gather(jnp.concatenate(pieces, axis=1), "wide", axis=0, tiled=True)
        offsets = [sum(widths[:k]) for k in range(len(widths))]
        return [gathered[:, o:o + w] for o, w in zip(offsets, widths)]

    attn_pieces = [wq, wk, wv, wo.T]
    attn_gathered = lax.all_gather(jnp.concatenate(attn_pieces, axis=1), "wide", axis=0, tiled=True)
    wo_t = attn_gathered[:, 3 * attn_width:]
    wg_all, wu_all, wd_t = gather_pieces([wg, wu, wd.T])

    id_blocks = []
    for step_back in range(REACH, 0, -1):
        got = shifted(segment_ids, "wide", step_back)
        id_blocks.append(jnp.where(wide_rank >= step_back, got, -1))
    id_blocks.append(segment_ids)
    window_ids = jnp.concatenate(id_blocks, axis=0)
    window_len = window_ids.shape[0]
    lead = REACH * tok_rows
    window_index = jnp.arange(window_len, dtype=jnp.int32)
    same = window_ids[None, :] == segment_ids[:, None]
    earlier = same & (window_index[None, :] < lead + local_index[:, None])
    positions = jnp.sum(earlier.astype(jnp.int32), axis=1)

    pairs_per_chip = 2
    chips_back = REACH // pairs_per_chip
    partner_rank = wide_rank ^ 1
    first_core = (wide_rank % pairs_per_chip) == 0
    block_ids = [
        wide_rank - pairs_per_chip * chips_back,
        jnp.where(first_core, partner_rank - pairs_per_chip * chips_back, partner_rank),
    ]
    for step in range(chips_back - 1, 0, -1):
        block_ids += [wide_rank - pairs_per_chip * step, partner_rank - pairs_per_chip * step]
    block_ids += [wide_rank]
    key_index = (
        jnp.stack(block_ids)[:, None] * tok_rows + local_index[None, :]
    ).reshape(-1)
    query_index = wide_rank * tok_rows + local_index
    query_start = query_index - positions
    allowed = (key_index[None, :] >= query_start[:, None]) & (key_index[None, :] <= query_index[:, None])
    allowed, hidden_sent = lax.optimization_barrier((allowed, hidden_in))

    whole = swap_gather(hidden_sent, "narrow")
    normed = norm_rows(whole)
    local_width = attn_width
    head_count = local_width // HEAD_DIM

    projected = add_rows(normed, attn_gathered)
    q_proj = projected[:, :attn_width]
    k_proj = projected[:, attn_width:2 * attn_width]
    v_proj = projected[:, 2 * attn_width:3 * attn_width]
    queries = rotate(q_proj.reshape(tok_rows, head_count, HEAD_DIM), positions).astype(jnp.bfloat16)
    keys_rot = rotate(k_proj.reshape(tok_rows, head_count, HEAD_DIM), positions).astype(
        jnp.bfloat16
    )
    values = v_proj.astype(jnp.bfloat16).reshape(tok_rows, head_count, HEAD_DIM)
    packed = jnp.transpose(jnp.concatenate([keys_rot, values], axis=2), (1, 2, 0))
    line = [shifted(packed, "wide", pairs_per_chip * step) for step in range(1, chips_back + 1)]
    count = lax.axis_size("wide")
    partner = lax.ppermute(
        jnp.stack(line + [packed], axis=0), "wide", [(i, i ^ 1) for i in range(count)]
    )
    order = [line[chips_back - 1], jnp.where(first_core, partner[chips_back - 1], partner[chips_back])]
    for step in range(chips_back - 1, 0, -1):
        order += [line[step - 1], partner[step - 1]]
    order += [packed]
    kv_all = jnp.concatenate(order, axis=-1)
    score_scale = HEAD_DIM ** (-0.5)
    key_all = kv_all[:, :HEAD_DIM, :]
    value_all = kv_all[:, HEAD_DIM:, :]
    scores = (
        jnp.einsum("qhd,hdk->hqk", queries, key_all, preferred_element_type=jnp.float32)
        * score_scale
    )
    scores = jnp.where(allowed[None], scores, -1e30)
    row_peak = jnp.max(scores, axis=-1, keepdims=True)
    exps = jnp.where(allowed[None], jnp.exp(scores - row_peak), 0.0)
    attn_probs = (exps / jnp.sum(exps, axis=-1, keepdims=True)).astype(jnp.bfloat16)
    mixed = jnp.einsum("hqk,hdk->qhd", attn_probs, value_all, preferred_element_type=jnp.float32)
    attended = mixed.astype(jnp.bfloat16).reshape(tok_rows, local_width)
    narrow_count = lax.axis_size("narrow")
    attn_terms = jnp.einsum(
        "tc,goc->gto", attended, wo_t.reshape(narrow_count, -1, wo_t.shape[1]),
        preferred_element_type=jnp.float32,
    )
    attn_sum = swap_sum(attn_terms.astype(jnp.bfloat16), "narrow")
    first_res = (hidden_in.astype(jnp.float32) + attn_sum).astype(jnp.bfloat16)
    copies = jnp.broadcast_to(first_res[None], (narrow_count,) + first_res.shape)
    pieces_two = lax.all_to_all(copies, "narrow", 0, 0, tiled=True).astype(jnp.float32)
    center = pieces_two - jnp.mean(pieces_two, axis=(0, 2), keepdims=True)
    spread = jnp.mean(center * center, axis=(0, 2), keepdims=True)
    normed_two = (center * lax.rsqrt(spread + epsilon)).astype(jnp.bfloat16)

    def add_pieces(piece):
        return jnp.einsum(
            "gtc,gcu->tu", normed_two, piece.reshape(narrow_count, -1, piece.shape[1]),
            preferred_element_type=jnp.float32,
        )

    gate_proj = add_pieces(wg_all)
    up_proj = add_pieces(wu_all)
    hidden = (jax.nn.silu(gate_proj) * up_proj).astype(jnp.bfloat16)
    down_terms = jnp.einsum(
        "tc,goc->gto", hidden, wd_t.reshape(narrow_count, -1, wd_t.shape[1]),
        preferred_element_type=jnp.float32,
    )
    down_sum = swap_sum(down_terms.astype(jnp.bfloat16), "narrow")
    result = (first_res.astype(jnp.float32) + down_sum).astype(jnp.bfloat16)
    page_count = tok_rows // PAGE
    slots = page_table - wide_rank * page_count
    pairs = jnp.stack(
        [
            keys_rot.reshape(page_count, PAGE, local_width),
            values.reshape(page_count, PAGE, local_width),
        ],
        axis=0,
    )
    kv_cache = jnp.zeros_like(pairs).at[:, slots].set(pairs)
    return (result, kv_cache)


def solution(mesh):
    return jax.shard_map(
        per_device,
        mesh=mesh,
        in_specs=(
            P("wide", "narrow"),
            P("wide"),
            P("wide"),
            P("wide", "narrow"),
            P("wide", "narrow"),
            P("wide", "narrow"),
            P("narrow", "wide"),
            P("wide", "narrow"),
            P("wide", "narrow"),
            P("narrow", "wide"),
        ),
        out_specs=(P("wide", "narrow"), P(None, "wide", None, "narrow")),
        check_vma=False,
    )
```
